1024 devices in a mesh: ctx: 128 (over z, y), exp: 8 (over x, core).
Axes of the slice: x: 4, y: 8, z: 16, core: 2. Of those that a mesh axis runs over, the one named last changes fastest.
Arguments:
- scan_grad: bfloat16 [32768, 8192], P('ctx', 'exp'), may hold values from -6 to 6
- step_size: bfloat16 [32768, 8192], P('ctx', 'exp'), may hold values from 0.3 to 4.5, as said below
- scan_input: bfloat16 [32768, 8192], P('ctx', 'exp'), may hold values from -6 to 6
- state_in: float32 [32768, 16], P('ctx'), may hold values from -2 to 2
- state_out: float32 [32768, 16], P('ctx'), may hold values from -0.5 to 0.5
- decay_rate: float32 [16, 8192], P(None, 'exp'), may hold values from -1 to 0, as said below
- skip_gain: float32 [8192], P('exp'), may hold values from 0.5 to 1.5
Outputs:
- scan_input_grad: bfloat16 [32768, 8192], P('ctx', 'exp')
- state_in_grad: float32 [16, 32768], P(None, ('ctx', 'exp'))
The draws below stay inside these ranges and needn't reach their ends.
Inputs may be any that keep to these rules, and one draw needn't show every extreme that they name: `step_size`: Positive. `decay_rate`: Negative.
All inputs are finite; a program needn't handle non-finite values.
Results may differ from the reference program's by a relative error of at most 0.0015.
Values sent between devices are 32-bit elements; how exact they have to be, the bound alone decides.
No kernel may reach another device: no remote copies, remote signals or barrier semaphores. Data moves between devices by JAX's collectives and lax.ppermute only.
A program may use at most 64 MiB of HBM per device.

```python
import math
import jax
import jax.numpy as jnp
from jax import lax

INNER = 8192
STATE = 16
TOK_DEV = 256
TOKENS = 32768


def draw_step_size(key, part):
    base_key, block_key, mixed_key = jax.random.split(key, 3)
    base = jax.random.uniform(base_key, (TOKENS, INNER), jnp.float32, 0.5, 1.5)
    factor = jnp.exp(jax.random.uniform(block_key, (TOKENS // TOK_DEV, 1, 1), jnp.float32, 0.0, math.log(3.0)))
    mixed = jnp.exp(jax.random.uniform(mixed_key, (TOKENS // TOK_DEV, 1, INNER), jnp.float32, -math.log(3.0), math.log(3.0)))
    shaped = base.reshape(TOKENS // TOK_DEV, TOK_DEV, INNER) * factor * mixed
    shaped = jnp.clip(shaped, 0.3, 4.5)
    return shaped.reshape(TOKENS, INNER).astype(jnp.bfloat16)


def draw_decay_rate(key, part):
    keys = jax.random.split(key, 5)
    spread = jnp.exp(jax.random.uniform(keys[0], (STATE, INNER), jnp.float32, 0.0, math.log(4.0)))
    fast_rate = jnp.exp(jax.random.uniform(keys[1], (1, INNER), jnp.float32, math.log(1.0 / 160.0), math.log(1.0 / 40.0)))
    slow_rate = jnp.exp(jax.random.uniform(keys[2], (1, INNER), jnp.float32, math.log(0.005), math.log(0.05))) / TOKENS
    middle_rate = jnp.exp(jax.random.uniform(keys[4], (1, INNER), jnp.float32, math.log(0.05), math.log(0.5))) / TOK_DEV
    chooser = jax.random.uniform(keys[3], (1, INNER), jnp.float32, 0.0, 1.0)
    fast_cut = 0.4
    middle_cut = 0.6
    picked = jnp.where(chooser < fast_cut, fast_rate, jnp.where(chooser < middle_cut, middle_rate, slow_rate))
    return -(picked * spread)


def block_levels(stream_key, shape, pieces, low, largest):
    gain = 1.0
    for axis_at, parts in pieces:
        draws = jax.random.uniform(jax.random.fold_in(jax.random.fold_in(stream_key, 6), axis_at), (parts,), jnp.float32, low / len(pieces), largest / len(pieces))
        gain = gain * jnp.repeat(jnp.exp(draws), shape[axis_at] // parts).reshape((-1,) + (1,) * (len(shape) - 1 - axis_at))
    return gain


def scatter_about(key, extent, width, reach, cuts=(), dtype=jnp.bfloat16):
    values = width * jax.random.normal(key, extent, jnp.float32)
    if cuts:
        values = values * block_levels(key, extent, cuts, -0.22, 0.18)
    return jnp.clip(values, -reach, reach).astype(dtype)


def setup_inputs(seed: int = 0) -> dict:
    key_list = jax.random.split(jax.random.key(seed), 8)
    scan_grad = scatter_about(key_list[0], (TOKENS, INNER), 1.0, 6.0, ((0, 128), (1, 8)))
    step_size = draw_step_size(jax.random.fold_in(key_list[7], 71), 0)
    scan_input = scatter_about(key_list[2], (TOKENS, INNER), 1.0, 6.0, ((0, 128), (1, 8)))
    state_in = scatter_about(key_list[3], (TOKENS, STATE), 0.125, 2.0, ((0, 128),), jnp.float32)
    state_out = scatter_about(key_list[4], (TOKENS, STATE), 0.03125, 0.5, ((0, 128),), jnp.float32)
    decay_rate = draw_decay_rate(jax.random.fold_in(key_list[7], 71), 0)
    skip_gain = jnp.clip(1.0 + 0.1 * jax.random.normal(key_list[6], (INNER,), jnp.float32), 0.5, 1.5)
    return dict(scan_grad=scan_grad, step_size=step_size, scan_input=scan_input, state_in=state_in, state_out=state_out, decay_rate=decay_rate, skip_gain=skip_gain)


def reference(scan_grad, step_size, scan_input, state_in, state_out, decay_rate, skip_gain):

    def step_back(incoming, row_data):
        grad_row, step_row, input_row, in_row, out_row = row_data
        grad_row = grad_row.astype(jnp.float32)
        step_row = step_row.astype(jnp.float32)
        input_row = input_row.astype(jnp.float32)
        adjoint = out_row[:, None] * grad_row[None, :] + incoming
        result = step_row * lax.optimization_barrier(jnp.sum(in_row[:, None] * adjoint, axis=0)) + skip_gain * grad_row
        b_grad = lax.optimization_barrier(jnp.sum(adjoint * (step_row * input_row)[None, :], axis=1))
        return (jnp.exp(step_row[None, :] * decay_rate) * adjoint, (result.astype(jnp.bfloat16), b_grad))
    start_state = jnp.zeros((STATE, INNER), jnp.float32)
    _, outputs = lax.scan(step_back, start_state, (scan_grad, step_size, scan_input, state_in, state_out), reverse=True)
    grads_all, b_all = outputs
    state_in_grad = jnp.transpose(b_all) * (1.0 / math.sqrt(INNER))
    return (grads_all, state_in_grad)
```

```python
import math

import jax
import jax.numpy as jnp
from jax import lax
from jax.experimental import pallas as pl
from jax.experimental.pallas import tpu as pltpu
from jax.sharding import PartitionSpec as P

LANES = 128


def tiled(column_block, tiles):
    return jnp.concatenate([column_block] * tiles, axis=1)


def summary_kernel(g_ref, s_ref, outb_ref, a_ref, sum_ref, tot_ref, gf, sf):
    rows, channels = g_ref.shape
    tiles = channels // LANES
    gf[...] = g_ref[...].astype(jnp.float32)
    sf[...] = s_ref[...].astype(jnp.float32)
    tot_ref[...] = jnp.sum(sf[...], axis=0, keepdims=True)
    a = a_ref[...]

    def body(i, incoming):
        t = rows - 1 - i
        g_row = gf[pl.ds(t, 1), :]
        s_row = sf[pl.ds(t, 1), :]
        adjoint = tiled(outb_ref[t], tiles) * g_row + incoming
        return jnp.exp(s_row * a) * adjoint

    sum_ref[...] = lax.fori_loop(0, rows, body, jnp.zeros(a.shape, jnp.float32), unroll=8)


def sweep_kernel(
    g_ref, s_ref, x_ref, inb_ref, outb_ref, a_ref, skip_ref, inc_ref,
    res_ref, bp_ref, gf, sf, wf, rf,
):
    rows, channels = g_ref.shape
    tiles = channels // LANES
    gf[...] = g_ref[...].astype(jnp.float32)
    sf[...] = s_ref[...].astype(jnp.float32)
    wf[...] = sf[...] * x_ref[...].astype(jnp.float32)
    a = a_ref[...]
    skip = skip_ref[...]

    def body(i, incoming):
        t = rows - 1 - i
        g_row = gf[pl.ds(t, 1), :]
        s_row = sf[pl.ds(t, 1), :]
        w_row = wf[pl.ds(t, 1), :]
        adjoint = tiled(outb_ref[t], tiles) * g_row + incoming
        mixed = jnp.sum(tiled(inb_ref[t], tiles) * adjoint, axis=0, keepdims=True)
        rf[pl.ds(t, 1), :] = s_row * mixed + skip * g_row
        weighted = adjoint * w_row
        part = weighted[:, 0:LANES]
        for k in range(1, tiles):
            part = part + weighted[:, k * LANES:(k + 1) * LANES]
        bp_ref[t] = part
        return jnp.exp(s_row * a) * adjoint

    lax.fori_loop(0, rows, body, inc_ref[...], unroll=8)
    res_ref[...] = rf[...].astype(res_ref.dtype)


def vmem_spec():
    return pl.BlockSpec(memory_space=pltpu.VMEM)


def shard_summary(scan_grad, step_size, out_b, decay_rate):
    rows, channels = scan_grad.shape
    return pl.pallas_call(
        summary_kernel,
        out_shape=(
            jax.ShapeDtypeStruct(decay_rate.shape, jnp.float32),
            jax.ShapeDtypeStruct((1, channels), jnp.float32),
        ),
        in_specs=[vmem_spec()] * 4,
        out_specs=(vmem_spec(), vmem_spec()),
        scratch_shapes=[pltpu.VMEM((rows, channels), jnp.float32)] * 2,
        cost_estimate=pl.CostEstimate(
            flops=6 * rows * decay_rate.size,
            transcendentals=rows * decay_rate.size,
            bytes_accessed=4 * rows * channels + 4 * out_b.size,
        ),
    )(scan_grad, step_size, out_b, decay_rate)


def shard_sweep(scan_grad, step_size, scan_input, in_b, out_b, decay_rate, skip_gain, incoming):
    rows, channels = scan_grad.shape
    states = decay_rate.shape[0]
    return pl.pallas_call(
        sweep_kernel,
        out_shape=(
            jax.ShapeDtypeStruct((rows, channels), jnp.bfloat16),
            jax.ShapeDtypeStruct((rows, states, LANES), jnp.float32),
        ),
        in_specs=[vmem_spec()] * 8,
        out_specs=(vmem_spec(), vmem_spec()),
        scratch_shapes=[pltpu.VMEM((rows, channels), jnp.float32)] * 4,
        cost_estimate=pl.CostEstimate(
            flops=12 * rows * decay_rate.size,
            transcendentals=rows * decay_rate.size,
            bytes_accessed=8 * rows * channels + 4 * (in_b.size + out_b.size) * 2,
        ),
    )(scan_grad, step_size, scan_input, in_b, out_b, decay_rate, skip_gain, incoming)


def carry_in(summary, total, decay_rate):
    size = lax.axis_size("ctx")
    states = summary.shape[0]
    packed = jnp.concatenate([summary, total], axis=0)
    packed = lax.ppermute(packed, "ctx", [(q, q - 1) for q in range(1, size)])
    reach = 1
    while reach < size:
        got = lax.ppermute(packed, "ctx", [(q, q - reach) for q in range(reach, size)])
        own_s, own_r = packed[:states], packed[states:]
        new_s = own_s + jnp.exp(decay_rate * own_r) * got[:states]
        packed = jnp.concatenate([new_s, own_r + got[states:]], axis=0)
        reach *= 2
    return packed[:states]


def shards(scan_grad, step_size, scan_input, state_in, state_out, decay_rate, skip_gain):
    rows = scan_grad.shape[0]
    states = state_in.shape[1]
    in_b = jnp.broadcast_to(state_in[:, :, None], (rows, states, LANES))
    out_b = jnp.broadcast_to(state_out[:, :, None], (rows, states, LANES))
    summary, total = shard_summary(scan_grad, step_size, out_b, decay_rate)
    carried = carry_in(summary, total, decay_rate)
    scan_input_grad, b_part = shard_sweep(
        scan_grad, step_size, scan_input, in_b, out_b, decay_rate, skip_gain[None, :], carried
    )
    all_channels = scan_grad.shape[1] * lax.axis_size("exp")
    b_term = jnp.transpose(jnp.sum(b_part, axis=2)) * (1.0 / math.sqrt(all_channels))
    state_in_grad = lax.psum_scatter(b_term, "exp", scatter_dimension=1, tiled=True)
    return (scan_input_grad, state_in_grad)


def solution(mesh):
    in_specs = (
        P("ctx", "exp"),
        P("ctx", "exp"),
        P("ctx", "exp"),
        P("ctx", None),
        P("ctx", None),
        P(None, "exp"),
        P("exp"),
    )
    out_specs = (P("ctx", "exp"), P(None, ("ctx", "exp")))
    return jax.shard_map(shards, mesh=mesh, in_specs=in_specs, out_specs=out_specs, check_vma=False)
```

```python
import math

import jax
import jax.numpy as jnp
from jax import lax
from jax.experimental import pallas as pl
from jax.experimental.pallas import tpu as pltpu
from jax.sharding import PartitionSpec as P

LANES = 128


def tiled(column_block, tiles):
    return jnp.concatenate([column_block] * tiles, axis=1)


def summary_kernel(g_ref, s_ref, outb_ref, a_ref, sum_ref, tot_ref, gf, sf):
    rows, channels = g_ref.shape
    tiles = channels // LANES
    gf[...] = g_ref[...].astype(jnp.float32)
    sf[...] = s_ref[...].astype(jnp.float32)
    tot_ref[...] = jnp.sum(sf[...], axis=0, keepdims=True)
    a = a_ref[...]

    def body(i, incoming):
        t = rows - 1 - i
        g_row = gf[pl.ds(t, 1), :]
        s_row = sf[pl.ds(t, 1), :]
        adjoint = tiled(outb_ref[t], tiles) * g_row + incoming
        return jnp.exp(s_row * a) * adjoint

    sum_ref[...] = lax.fori_loop(0, rows, body, jnp.zeros(a.shape, jnp.float32), unroll=8)


def sweep_kernel(
    g_ref, s_ref, x_ref, inb_ref, outb_ref, a_ref, skip_ref, inc_ref,
    res_ref, bp_ref, gf, sf, wf, rf,
):
    rows, channels = g_ref.shape
    tiles = channels // LANES
    gf[...] = g_ref[...].astype(jnp.float32)
    sf[...] = s_ref[...].astype(jnp.float32)
    wf[...] = sf[...] * x_ref[...].astype(jnp.float32)
    a = a_ref[...]
    skip = skip_ref[...]

    def body(i, incoming):
        t = rows - 1 - i
        g_row = gf[pl.ds(t, 1), :]
        s_row = sf[pl.ds(t, 1), :]
        w_row = wf[pl.ds(t, 1), :]
        adjoint = tiled(outb_ref[t], tiles) * g_row + incoming
        mixed = jnp.sum(tiled(inb_ref[t], tiles) * adjoint, axis=0, keepdims=True)
        rf[pl.ds(t, 1), :] = s_row * mixed + skip * g_row
        weighted = adjoint * w_row
        part = weighted[:, 0:LANES]
        for k in range(1, tiles):
            part = part + weighted[:, k * LANES:(k + 1) * LANES]
        bp_ref[t] = part
        return jnp.exp(s_row * a) * adjoint

    lax.fori_loop(0, rows, body, inc_ref[...], unroll=8)
    res_ref[...] = rf[...].astype(res_ref.dtype)


def vmem_spec():
    return pl.BlockSpec(memory_space=pltpu.VMEM)


def shard_summary(scan_grad, step_size, out_b, decay_rate):
    rows, channels = scan_grad.shape
    return pl.pallas_call(
        summary_kernel,
        out_shape=(
            jax.ShapeDtypeStruct(decay_rate.shape, jnp.float32),
            jax.ShapeDtypeStruct((1, channels), jnp.float32),
        ),
        in_specs=[vmem_spec()] * 4,
        out_specs=(vmem_spec(), vmem_spec()),
        scratch_shapes=[pltpu.VMEM((rows, channels), jnp.float32)] * 2,
        cost_estimate=pl.CostEstimate(
            flops=6 * rows * decay_rate.size,
            transcendentals=rows * decay_rate.size,
            bytes_accessed=4 * rows * channels + 4 * out_b.size,
        ),
    )(scan_grad, step_size, out_b, decay_rate)


def shard_sweep(scan_grad, step_size, scan_input, in_b, out_b, decay_rate, skip_gain, incoming):
    rows, channels = scan_grad.shape
    states = decay_rate.shape[0]
    return pl.pallas_call(
        sweep_kernel,
        out_shape=(
            jax.ShapeDtypeStruct((rows, channels), jnp.bfloat16),
            jax.ShapeDtypeStruct((rows, states, LANES), jnp.float32),
        ),
        in_specs=[vmem_spec()] * 8,
        out_specs=(vmem_spec(), vmem_spec()),
        scratch_shapes=[pltpu.VMEM((rows, channels), jnp.float32)] * 4,
        cost_estimate=pl.CostEstimate(
            flops=12 * rows * decay_rate.size,
            transcendentals=rows * decay_rate.size,
            bytes_accessed=8 * rows * channels + 4 * (in_b.size + out_b.size) * 2,
        ),
    )(scan_grad, step_size, scan_input, in_b, out_b, decay_rate, skip_gain, incoming)


def carry_in(summary, total, decay_rate):
    size = lax.axis_size("ctx")
    states = summary.shape[0]
    packed = jnp.concatenate([summary, total], axis=0)
    packed = lax.ppermute(packed, "ctx", [(q, q - 1) for q in range(1, size)])
    reach = 1
    while reach < size:
        got = lax.ppermute(packed, "ctx", [(q, q - reach) for q in range(reach, size)])
        own_s, own_r = packed[:states], packed[states:]
        new_s = own_s + jnp.exp(decay_rate * own_r) * got[:states]
        packed = jnp.concatenate([new_s, own_r + got[states:]], axis=0)
        reach *= 2
    return packed[:states]


def halving_sum(block, axis):
    size = lax.axis_size(axis)
    me = lax.axis_index(axis)
    bit = size // 2
    while bit >= 1:
        half = block.shape[1] // 2
        low, high = block[:, :half], block[:, half:]
        upper = (me // bit) % 2 == 1
        keep = jnp.where(upper, high, low)
        send = jnp.where(upper, low, high)
        got = lax.ppermute(send, axis, [(e, e ^ bit) for e in range(size)])
        block = keep + got
        bit //= 2
    return block


def shards(scan_grad, step_size, scan_input, state_in, state_out, decay_rate, skip_gain):
    rows = scan_grad.shape[0]
    states = state_in.shape[1]
    in_b = jnp.broadcast_to(state_in[:, :, None], (rows, states, LANES))
    out_b = jnp.broadcast_to(state_out[:, :, None], (rows, states, LANES))
    summary, total = shard_summary(scan_grad, step_size, out_b, decay_rate)
    carried = carry_in(summary, total, decay_rate)
    scan_input_grad, b_part = shard_sweep(
        scan_grad, step_size, scan_input, in_b, out_b, decay_rate, skip_gain[None, :], carried
    )
    all_channels = scan_grad.shape[1] * lax.axis_size("exp")
    b_term = jnp.transpose(jnp.sum(b_part, axis=2)) * (1.0 / math.sqrt(all_channels))
    state_in_grad = halving_sum(b_term, "exp")
    return (scan_input_grad, state_in_grad)


def solution(mesh):
    in_specs = (
        P("ctx", "exp"),
        P("ctx", "exp"),
        P("ctx", "exp"),
        P("ctx", None),
        P("ctx", None),
        P(None, "exp"),
        P("exp"),
    )
    out_specs = (P("ctx", "exp"), P(None, ("ctx", "exp")))
    return jax.shard_map(shards, mesh=mesh, in_specs=in_specs, out_specs=out_specs, check_vma=False)
```

```python
import math

import jax
import jax.numpy as jnp
from jax import lax
from jax.experimental import pallas as pl
from jax.experimental.pallas import tpu as pltpu
from jax.sharding import PartitionSpec as P

LANES = 128


def tiled(column_block, tiles):
    return jnp.concatenate([column_block] * tiles, axis=1)


def summary_kernel(g_ref, s_ref, outb_ref, a_ref, sum_ref, tot_ref, gf, sf):
    rows, channels = g_ref.shape
    tiles = channels // LANES
    gf[...] = g_ref[...].astype(jnp.float32)
    sf[...] = s_ref[...].astype(jnp.float32)
    tot_ref[...] = jnp.sum(sf[...], axis=0, keepdims=True)
    a = a_ref[...]

    def body(i, incoming):
        t = rows - 1 - i
        g_row = gf[pl.ds(t, 1), :]
        s_row = sf[pl.ds(t, 1), :]
        adjoint = tiled(outb_ref[t], tiles) * g_row + incoming
        return jnp.exp(s_row * a) * adjoint

    sum_ref[...] = lax.fori_loop(0, rows, body, jnp.zeros(a.shape, jnp.float32), unroll=8)


def sweep_kernel(
    g_ref, s_ref, x_ref, inb_ref, outb_ref, a_ref, skip_ref, inc_ref,
    res_ref, bp_ref, gf, sf, wf, rf,
):
    rows, channels = g_ref.shape
    tiles = channels // LANES
    gf[...] = g_ref[...].astype(jnp.float32)
    sf[...] = s_ref[...].astype(jnp.float32)
    wf[...] = sf[...] * x_ref[...].astype(jnp.float32)
    a = a_ref[...]
    skip = skip_ref[...]

    def body(i, incoming):
        t = rows - 1 - i
        g_row = gf[pl.ds(t, 1), :]
        s_row = sf[pl.ds(t, 1), :]
        w_row = wf[pl.ds(t, 1), :]
        adjoint = tiled(outb_ref[t], tiles) * g_row + incoming
        mixed = jnp.sum(tiled(inb_ref[t], tiles) * adjoint, axis=0, keepdims=True)
        rf[pl.ds(t, 1), :] = s_row * mixed + skip * g_row
        weighted = adjoint * w_row
        part = weighted[:, 0:LANES]
        for k in range(1, tiles):
            part = part + weighted[:, k * LANES:(k + 1) * LANES]
        bp_ref[t] = part
        return jnp.exp(s_row * a) * adjoint

    lax.fori_loop(0, rows, body, inc_ref[...], unroll=8)
    res_ref[...] = rf[...].astype(res_ref.dtype)


def vmem_spec():
    return pl.BlockSpec(memory_space=pltpu.VMEM)


def shard_summary(scan_grad, step_size, out_b, decay_rate):
    rows, channels = scan_grad.shape
    return pl.pallas_call(
        summary_kernel,
        out_shape=(
            jax.ShapeDtypeStruct(decay_rate.shape, jnp.float32),
            jax.ShapeDtypeStruct((1, channels), jnp.float32),
        ),
        in_specs=[vmem_spec()] * 4,
        out_specs=(vmem_spec(), vmem_spec()),
        scratch_shapes=[pltpu.VMEM((rows, channels), jnp.float32)] * 2,
        cost_estimate=pl.CostEstimate(
            flops=6 * rows * decay_rate.size,
            transcendentals=rows * decay_rate.size,
            bytes_accessed=4 * rows * channels + 4 * out_b.size,
        ),
    )(scan_grad, step_size, out_b, decay_rate)


def shard_sweep(scan_grad, step_size, scan_input, in_b, out_b, decay_rate, skip_gain, incoming):
    rows, channels = scan_grad.shape
    states = decay_rate.shape[0]
    return pl.pallas_call(
        sweep_kernel,
        out_shape=(
            jax.ShapeDtypeStruct((rows, channels), jnp.bfloat16),
            jax.ShapeDtypeStruct((rows, states, LANES), jnp.float32),
        ),
        in_specs=[vmem_spec()] * 8,
        out_specs=(vmem_spec(), vmem_spec()),
        scratch_shapes=[pltpu.VMEM((rows, channels), jnp.float32)] * 4,
        cost_estimate=pl.CostEstimate(
            flops=12 * rows * decay_rate.size,
            transcendentals=rows * decay_rate.size,
            bytes_accessed=8 * rows * channels + 4 * (in_b.size + out_b.size) * 2,
        ),
    )(scan_grad, step_size, scan_input, in_b, out_b, decay_rate, skip_gain, incoming)


def carry_in(summary, total, decay_rate, radix=4):
    size = lax.axis_size("ctx")
    states = summary.shape[0]
    packed = jnp.concatenate([summary, total], axis=0)
    own = None
    covered, stride, count = 0, 1, radix
    while covered < size - 1:
        pieces = [] if own is None else [own]
        for j in range(1, count + 1):
            shift = j * stride
            if shift >= size:
                break
            source = packed if own is None else own
            pieces.append(
                lax.ppermute(source, "ctx", [(q, q - shift) for q in range(shift, size)])
            )
        acc_s, acc_r = pieces[-1][:states], pieces[-1][states:]
        for piece in pieces[-2::-1]:
            acc_s = piece[:states] + jnp.exp(decay_rate * piece[states:]) * acc_s
            acc_r = piece[states:] + acc_r
        own = jnp.concatenate([acc_s, acc_r], axis=0)
        covered = covered + (len(pieces) - (0 if covered == 0 else 1)) * stride
        stride = covered
        count = min(radix - 1, -(-(size - 1) // covered) - 1)
    return own[:states]


def halving_sum(block, axis):
    size = lax.axis_size(axis)
    me = lax.axis_index(axis)
    bit = size // 2
    while bit >= 1:
        half = block.shape[1] // 2
        low, high = block[:, :half], block[:, half:]
        upper = (me // bit) % 2 == 1
        keep = jnp.where(upper, high, low)
        send = jnp.where(upper, low, high)
        got = lax.ppermute(send, axis, [(e, e ^ bit) for e in range(size)])
        block = keep + got
        bit //= 2
    return block


def shards(scan_grad, step_size, scan_input, state_in, state_out, decay_rate, skip_gain):
    rows = scan_grad.shape[0]
    states = state_in.shape[1]
    in_b = jnp.broadcast_to(state_in[:, :, None], (rows, states, LANES))
    out_b = jnp.broadcast_to(state_out[:, :, None], (rows, states, LANES))
    summary, total = shard_summary(scan_grad, step_size, out_b, decay_rate)
    carried = carry_in(summary, total, decay_rate)
    scan_input_grad, b_part = shard_sweep(
        scan_grad, step_size, scan_input, in_b, out_b, decay_rate, skip_gain[None, :], carried
    )
    all_channels = scan_grad.shape[1] * lax.axis_size("exp")
    b_term = jnp.transpose(jnp.sum(b_part, axis=2)) * (1.0 / math.sqrt(all_channels))
    state_in_grad = halving_sum(b_term, "exp")
    return (scan_input_grad, state_in_grad)


def solution(mesh):
    in_specs = (
        P("ctx", "exp"),
        P("ctx", "exp"),
        P("ctx", "exp"),
        P("ctx", None),
        P("ctx", None),
        P(None, "exp"),
        P("exp"),
    )
    out_specs = (P("ctx", "exp"), P(None, ("ctx", "exp")))
    return jax.shard_map(shards, mesh=mesh, in_specs=in_specs, out_specs=out_specs, check_vma=False)
```

```python
import math

import jax
import jax.numpy as jnp
from jax import lax
from jax.experimental import pallas as pl
from jax.experimental.pallas import tpu as pltpu
from jax.sharding import PartitionSpec as P

LANES = 128


def tiled(column_block, tiles):
    return jnp.concatenate([column_block] * tiles, axis=1)


def summary_kernel(g_ref, s_ref, outb_ref, a_ref, sum_ref, tot_ref, gf, sf):
    rows, channels = g_ref.shape
    tiles = channels // LANES
    gf[...] = g_ref[...].astype(jnp.float32)
    sf[...] = s_ref[...].astype(jnp.float32)
    tot_ref[...] = jnp.sum(sf[...], axis=0, keepdims=True)
    a = a_ref[...]

    def body(i, incoming):
        t = rows - 1 - i
        g_row = gf[pl.ds(t, 1), :]
        s_row = sf[pl.ds(t, 1), :]
        adjoint = tiled(outb_ref[t], tiles) * g_row + incoming
        return jnp.exp(s_row * a) * adjoint

    sum_ref[...] = lax.fori_loop(0, rows, body, jnp.zeros(a.shape, jnp.float32), unroll=8)


def sweep_kernel(
    g_ref, s_ref, x_ref, inb_ref, outb_ref, a_ref, skip_ref, inc_ref,
    res_ref, bp_ref, gf, sf, wf, rf,
):
    rows, channels = g_ref.shape
    tiles = channels // LANES
    gf[...] = g_ref[...].astype(jnp.float32)
    sf[...] = s_ref[...].astype(jnp.float32)
    wf[...] = sf[...] * x_ref[...].astype(jnp.float32)
    a = a_ref[...]
    skip = skip_ref[...]

    def body(i, incoming):
        t = rows - 1 - i
        g_row = gf[pl.ds(t, 1), :]
        s_row = sf[pl.ds(t, 1), :]
        w_row = wf[pl.ds(t, 1), :]
        adjoint = tiled(outb_ref[t], tiles) * g_row + incoming
        mixed = jnp.sum(tiled(inb_ref[t], tiles) * adjoint, axis=0, keepdims=True)
        rf[pl.ds(t, 1), :] = s_row * mixed + skip * g_row
        weighted = adjoint * w_row
        part = weighted[:, 0:LANES]
        for k in range(1, tiles):
            part = part + weighted[:, k * LANES:(k + 1) * LANES]
        bp_ref[t] = part
        return jnp.exp(s_row * a) * adjoint

    lax.fori_loop(0, rows, body, inc_ref[...], unroll=8)
    res_ref[...] = rf[...].astype(res_ref.dtype)


def vmem_spec():
    return pl.BlockSpec(memory_space=pltpu.VMEM)


def shard_summary(scan_grad, step_size, out_b, decay_rate):
    rows, channels = scan_grad.shape
    return pl.pallas_call(
        summary_kernel,
        out_shape=(
            jax.ShapeDtypeStruct(decay_rate.shape, jnp.float32),
            jax.ShapeDtypeStruct((1, channels), jnp.float32),
        ),
        in_specs=[vmem_spec()] * 4,
        out_specs=(vmem_spec(), vmem_spec()),
        scratch_shapes=[pltpu.VMEM((rows, channels), jnp.float32)] * 2,
        cost_estimate=pl.CostEstimate(
            flops=6 * rows * decay_rate.size,
            transcendentals=rows * decay_rate.size,
            bytes_accessed=4 * rows * channels + 4 * out_b.size,
        ),
    )(scan_grad, step_size, out_b, decay_rate)


def shard_sweep(scan_grad, step_size, scan_input, in_b, out_b, decay_rate, skip_gain, incoming):
    rows, channels = scan_grad.shape
    states = decay_rate.shape[0]
    return pl.pallas_call(
        sweep_kernel,
        out_shape=(
            jax.ShapeDtypeStruct((rows, channels), jnp.bfloat16),
            jax.ShapeDtypeStruct((rows, states, LANES), jnp.float32),
        ),
        in_specs=[vmem_spec()] * 8,
        out_specs=(vmem_spec(), vmem_spec()),
        scratch_shapes=[pltpu.VMEM((rows, channels), jnp.float32)] * 4,
        cost_estimate=pl.CostEstimate(
            flops=12 * rows * decay_rate.size,
            transcendentals=rows * decay_rate.size,
            bytes_accessed=8 * rows * channels + 4 * (in_b.size + out_b.size) * 2,
        ),
    )(scan_grad, step_size, scan_input, in_b, out_b, decay_rate, skip_gain, incoming)


def gathered_suffix(pieces, me, decay_rate):
    count, packed_rows, _ = pieces.shape
    states = packed_rows - 1
    summaries, totals = pieces[:, :states], pieces[:, states:]
    index = lax.broadcasted_iota(jnp.int32, (count, count, 1, 1), 0)
    inner = lax.broadcasted_iota(jnp.int32, (count, count, 1, 1), 1)
    between = jnp.where((inner > me) & (inner < index), totals[None], 0.0)
    before = jnp.where(inner < index, totals[None], 0.0)
    reach_after = jnp.sum(between, axis=1)
    reach_all = jnp.sum(before, axis=1)
    later = (lax.broadcasted_iota(jnp.int32, (count, 1, 1), 0) > me)
    after_s = jnp.sum(
        jnp.where(later, jnp.exp(decay_rate[None] * reach_after) * summaries, 0.0), axis=0
    )
    after_r = jnp.sum(jnp.where(later, totals, 0.0), axis=0)
    all_s = jnp.sum(jnp.exp(decay_rate[None] * reach_all) * summaries, axis=0)
    all_r = jnp.sum(totals, axis=0)
    return (after_s, after_r), (all_s, all_r)


def carry_in(summary, total, decay_rate):
    packed = jnp.concatenate([summary, total], axis=0)
    near = lax.all_gather(packed, "ctx_in")
    (near_s, near_r), (group_s, group_r) = gathered_suffix(
        near, lax.axis_index("ctx_in"), decay_rate
    )
    far = lax.all_gather(jnp.concatenate([group_s, group_r], axis=0), "ctx_out")
    (far_s, _), _ = gathered_suffix(far, lax.axis_index("ctx_out"), decay_rate)
    return near_s + jnp.exp(decay_rate * near_r) * far_s


def halving_sum(block, axis):
    size = lax.axis_size(axis)
    me = lax.axis_index(axis)
    bit = size // 2
    while bit >= 1:
        half = block.shape[1] // 2
        low, high = block[:, :half], block[:, half:]
        upper = (me // bit) % 2 == 1
        keep = jnp.where(upper, high, low)
        send = jnp.where(upper, low, high)
        got = lax.ppermute(send, axis, [(e, e ^ bit) for e in range(size)])
        block = keep + got
        bit //= 2
    return block


def shards(scan_grad, step_size, scan_input, state_in, state_out, decay_rate, skip_gain):
    rows = scan_grad.shape[0]
    states = state_in.shape[1]
    in_b = jnp.broadcast_to(state_in[:, :, None], (rows, states, LANES))
    out_b = jnp.broadcast_to(state_out[:, :, None], (rows, states, LANES))
    summary, total = shard_summary(scan_grad, step_size, out_b, decay_rate)
    carried = carry_in(summary, total, decay_rate)
    scan_input_grad, b_part = shard_sweep(
        scan_grad, step_size, scan_input, in_b, out_b, decay_rate, skip_gain[None, :], carried
    )
    all_channels = scan_grad.shape[1] * lax.axis_size("exp")
    b_term = jnp.transpose(jnp.sum(b_part, axis=2)) * (1.0 / math.sqrt(all_channels))
    state_in_grad = halving_sum(b_term, "exp")
    return (scan_input_grad, state_in_grad)


def solution(mesh):
    ctx_size = mesh.shape["ctx"]
    inner = 8 if ctx_size % 8 == 0 else 1
    split = jax.sharding.Mesh(
        mesh.devices.reshape(ctx_size // inner, inner, mesh.shape["exp"]),
        ("ctx_out", "ctx_in", "exp"),
    )
    ctx = ("ctx_out", "ctx_in")
    in_specs = (
        P(ctx, "exp"),
        P(ctx, "exp"),
        P(ctx, "exp"),
        P(ctx, None),
        P(ctx, None),
        P(None, "exp"),
        P("exp"),
    )
    out_specs = (P(ctx, "exp"), P(None, ctx + ("exp",)))
    return jax.shard_map(shards, mesh=split, in_specs=in_specs, out_specs=out_specs, check_vma=False)
```

```python
import math

import jax
import jax.numpy as jnp
from jax import lax
from jax.experimental import pallas as pl
from jax.experimental.pallas import tpu as pltpu
from jax.sharding import PartitionSpec as P

LANES = 128


def tiled(column_block, tiles):
    return jnp.concatenate([column_block] * tiles, axis=1)


def summary_kernel(g_ref, s_ref, outb_ref, a_ref, sum_ref, tot_ref, gf, sf):
    rows, channels = g_ref.shape
    tiles = channels // LANES
    gf[...] = g_ref[...].astype(jnp.float32)
    sf[...] = s_ref[...].astype(jnp.float32)
    tot_ref[...] = jnp.sum(sf[...], axis=0, keepdims=True)
    a = a_ref[...]

    def body(i, incoming):
        t = rows - 1 - i
        g_row = gf[pl.ds(t, 1), :]
        s_row = sf[pl.ds(t, 1), :]
        adjoint = tiled(outb_ref[t], tiles) * g_row + incoming
        return jnp.exp(s_row * a) * adjoint

    sum_ref[...] = lax.fori_loop(0, rows, body, jnp.zeros(a.shape, jnp.float32), unroll=8)


def sweep_kernel(
    g_ref, s_ref, x_ref, inb_ref, outb_ref, a_ref, skip_ref, inc_ref,
    res_ref, bp_ref, gf, sf, wf, rf,
):
    rows, channels = g_ref.shape
    tiles = channels // LANES
    gf[...] = g_ref[...].astype(jnp.float32)
    sf[...] = s_ref[...].astype(jnp.float32)
    wf[...] = sf[...] * x_ref[...].astype(jnp.float32)
    a = a_ref[...]
    skip = skip_ref[...]

    def body(i, incoming):
        t = rows - 1 - i
        g_row = gf[pl.ds(t, 1), :]
        s_row = sf[pl.ds(t, 1), :]
        w_row = wf[pl.ds(t, 1), :]
        adjoint = tiled(outb_ref[t], tiles) * g_row + incoming
        mixed = jnp.sum(tiled(inb_ref[t], tiles) * adjoint, axis=0, keepdims=True)
        rf[pl.ds(t, 1), :] = s_row * mixed + skip * g_row
        weighted = adjoint * w_row
        part = weighted[:, 0:LANES]
        for k in range(1, tiles):
            part = part + weighted[:, k * LANES:(k + 1) * LANES]
        bp_ref[t] = part
        return jnp.exp(s_row * a) * adjoint

    lax.fori_loop(0, rows, body, inc_ref[...], unroll=8)
    res_ref[...] = rf[...].astype(res_ref.dtype)


def vmem_spec():
    return pl.BlockSpec(memory_space=pltpu.VMEM)


def shard_summary(scan_grad, step_size, out_b, decay_rate):
    rows, channels = scan_grad.shape
    return pl.pallas_call(
        summary_kernel,
        out_shape=(
            jax.ShapeDtypeStruct(decay_rate.shape, jnp.float32),
            jax.ShapeDtypeStruct((1, channels), jnp.float32),
        ),
        in_specs=[vmem_spec()] * 4,
        out_specs=(vmem_spec(), vmem_spec()),
        scratch_shapes=[pltpu.VMEM((rows, channels), jnp.float32)] * 2,
        cost_estimate=pl.CostEstimate(
            flops=6 * rows * decay_rate.size,
            transcendentals=rows * decay_rate.size,
            bytes_accessed=4 * rows * channels + 4 * out_b.size,
        ),
    )(scan_grad, step_size, out_b, decay_rate)


def shard_sweep(scan_grad, step_size, scan_input, in_b, out_b, decay_rate, skip_gain, incoming):
    rows, channels = scan_grad.shape
    states = decay_rate.shape[0]
    return pl.pallas_call(
        sweep_kernel,
        out_shape=(
            jax.ShapeDtypeStruct((rows, channels), jnp.bfloat16),
            jax.ShapeDtypeStruct((rows, states, LANES), jnp.float32),
        ),
        in_specs=[vmem_spec()] * 8,
        out_specs=(vmem_spec(), vmem_spec()),
        scratch_shapes=[pltpu.VMEM((rows, channels), jnp.float32)] * 4,
        cost_estimate=pl.CostEstimate(
            flops=12 * rows * decay_rate.size,
            transcendentals=rows * decay_rate.size,
            bytes_accessed=8 * rows * channels + 4 * (in_b.size + out_b.size) * 2,
        ),
    )(scan_grad, step_size, scan_input, in_b, out_b, decay_rate, skip_gain, incoming)


def carry_in(summary, total, decay_rate):
    size = lax.axis_size("ctx")
    states = summary.shape[0]
    packed = jnp.concatenate([summary, total], axis=0)
    packed = lax.ppermute(packed, "ctx", [(q, q - 1) for q in range(1, size)])
    reach = 1
    while reach < size:
        got = lax.ppermute(packed, "ctx", [(q, q - reach) for q in range(reach, size)])
        own_s, own_r = packed[:states], packed[states:]
        new_s = own_s + jnp.exp(decay_rate * own_r) * got[:states]
        packed = jnp.concatenate([new_s, own_r + got[states:]], axis=0)
        reach *= 2
    return packed[:states]


def exchange_sum(block, axis):
    size = lax.axis_size(axis)
    rows, columns = block.shape
    pieces = jnp.transpose(block.reshape(rows, size, columns // size), (1, 0, 2))
    got = lax.all_to_all(pieces, axis, 0, 0, tiled=True)
    return jnp.sum(got, axis=0)


def shards(scan_grad, step_size, scan_input, state_in, state_out, decay_rate, skip_gain):
    rows = scan_grad.shape[0]
    states = state_in.shape[1]
    in_b = jnp.broadcast_to(state_in[:, :, None], (rows, states, LANES))
    out_b = jnp.broadcast_to(state_out[:, :, None], (rows, states, LANES))
    summary, total = shard_summary(scan_grad, step_size, out_b, decay_rate)
    carried = carry_in(summary, total, decay_rate)
    scan_input_grad, b_part = shard_sweep(
        scan_grad, step_size, scan_input, in_b, out_b, decay_rate, skip_gain[None, :], carried
    )
    all_channels = scan_grad.shape[1] * lax.axis_size("exp")
    b_term = jnp.transpose(jnp.sum(b_part, axis=2)) * (1.0 / math.sqrt(all_channels))
    state_in_grad = exchange_sum(b_term, "exp")
    return (scan_input_grad, state_in_grad)


def solution(mesh):
    in_specs = (
        P("ctx", "exp"),
        P("ctx", "exp"),
        P("ctx", "exp"),
        P("ctx", None),
        P("ctx", None),
        P(None, "exp"),
        P("exp"),
    )
    out_specs = (P("ctx", "exp"), P(None, ("ctx", "exp")))
    return jax.shard_map(shards, mesh=mesh, in_specs=in_specs, out_specs=out_specs, check_vma=False)
```

```python
import math

import jax
import jax.numpy as jnp
from jax import lax
from jax.experimental import pallas as pl
from jax.experimental.pallas import tpu as pltpu
from jax.sharding import PartitionSpec as P

LANES = 128


def tiled(column_block, tiles):
    return jnp.concatenate([column_block] * tiles, axis=1)


def summary_kernel(g_ref, s_ref, outb_ref, a_ref, sum_ref, tot_ref, gf, sf):
    rows, channels = g_ref.shape
    tiles = channels // LANES
    gf[...] = g_ref[...].astype(jnp.float32)
    sf[...] = s_ref[...].astype(jnp.float32)
    tot_ref[...] = jnp.sum(sf[...], axis=0, keepdims=True)
    a = a_ref[...]

    def body(i, incoming):
        t = rows - 1 - i
        g_row = gf[pl.ds(t, 1), :]
        s_row = sf[pl.ds(t, 1), :]
        adjoint = tiled(outb_ref[t], tiles) * g_row + incoming
        return jnp.exp(s_row * a) * adjoint

    sum_ref[...] = lax.fori_loop(0, rows, body, jnp.zeros(a.shape, jnp.float32), unroll=8)


def sweep_kernel(
    g_ref, s_ref, x_ref, inb_ref, outb_ref, a_ref, skip_ref, inc_ref,
    res_ref, bp_ref, gf, sf, wf, rf,
):
    rows, channels = g_ref.shape
    tiles = channels // LANES
    gf[...] = g_ref[...].astype(jnp.float32)
    sf[...] = s_ref[...].astype(jnp.float32)
    wf[...] = sf[...] * x_ref[...].astype(jnp.float32)
    a = a_ref[...]
    skip = skip_ref[...]

    def body(i, incoming):
        t = rows - 1 - i
        g_row = gf[pl.ds(t, 1), :]
        s_row = sf[pl.ds(t, 1), :]
        w_row = wf[pl.ds(t, 1), :]
        adjoint = tiled(outb_ref[t], tiles) * g_row + incoming
        mixed = jnp.sum(tiled(inb_ref[t], tiles) * adjoint, axis=0, keepdims=True)
        rf[pl.ds(t, 1), :] = s_row * mixed + skip * g_row
        weighted = adjoint * w_row
        part = weighted[:, 0:LANES]
        for k in range(1, tiles):
            part = part + weighted[:, k * LANES:(k + 1) * LANES]
        bp_ref[t] = part
        return jnp.exp(s_row * a) * adjoint

    lax.fori_loop(0, rows, body, inc_ref[...], unroll=8)
    res_ref[...] = rf[...].astype(res_ref.dtype)


def vmem_spec():
    return pl.BlockSpec(memory_space=pltpu.VMEM)


def shard_summary(scan_grad, step_size, out_b, decay_rate):
    rows, channels = scan_grad.shape
    return pl.pallas_call(
        summary_kernel,
        out_shape=(
            jax.ShapeDtypeStruct(decay_rate.shape, jnp.float32),
            jax.ShapeDtypeStruct((1, channels), jnp.float32),
        ),
        in_specs=[vmem_spec()] * 4,
        out_specs=(vmem_spec(), vmem_spec()),
        scratch_shapes=[pltpu.VMEM((rows, channels), jnp.float32)] * 2,
        cost_estimate=pl.CostEstimate(
            flops=6 * rows * decay_rate.size,
            transcendentals=rows * decay_rate.size,
            bytes_accessed=4 * rows * channels + 4 * out_b.size,
        ),
    )(scan_grad, step_size, out_b, decay_rate)


def shard_sweep(scan_grad, step_size, scan_input, in_b, out_b, decay_rate, skip_gain, incoming):
    rows, channels = scan_grad.shape
    states = decay_rate.shape[0]
    return pl.pallas_call(
        sweep_kernel,
        out_shape=(
            jax.ShapeDtypeStruct((rows, channels), jnp.bfloat16),
            jax.ShapeDtypeStruct((rows, states, LANES), jnp.float32),
        ),
        in_specs=[vmem_spec()] * 8,
        out_specs=(vmem_spec(), vmem_spec()),
        scratch_shapes=[pltpu.VMEM((rows, channels), jnp.float32)] * 4,
        cost_estimate=pl.CostEstimate(
            flops=12 * rows * decay_rate.size,
            transcendentals=rows * decay_rate.size,
            bytes_accessed=8 * rows * channels + 4 * (in_b.size + out_b.size) * 2,
        ),
    )(scan_grad, step_size, scan_input, in_b, out_b, decay_rate, skip_gain, incoming)


def doubling_carry(summary, total, decay_rate):
    size = lax.axis_size("ctx")
    states = summary.shape[0]
    packed = jnp.concatenate([summary, total], axis=0)
    packed = lax.ppermute(packed, "ctx", [(q, q - 1) for q in range(1, size)])
    reach = 1
    while reach < size:
        got = lax.ppermute(packed, "ctx", [(q, q - reach) for q in range(reach, size)])
        own_s, own_r = packed[:states], packed[states:]
        new_s = own_s + jnp.exp(decay_rate * own_r) * got[:states]
        packed = jnp.concatenate([new_s, own_r + got[states:]], axis=0)
        reach *= 2
    return packed[:states]


def carry_in(summary, total, decay_rate):
    size = lax.axis_size("ctx")
    if size & (size - 1):
        return doubling_carry(summary, total, decay_rate)
    me = lax.axis_index("ctx")
    states = summary.shape[0]
    block_s, block_r = summary, total
    after_s, after_r = jnp.zeros_like(summary), jnp.zeros_like(total)
    bit = 1
    while bit < size:
        packed = jnp.concatenate([block_s, block_r], axis=0)
        got = lax.ppermute(packed, "ctx", [(q, q ^ bit) for q in range(size)])
        got_s, got_r = got[:states], got[states:]
        lower = (me // bit) % 2 == 0
        after_s = jnp.where(lower, after_s + jnp.exp(decay_rate * after_r) * got_s, after_s)
        after_r = jnp.where(lower, after_r + got_r, after_r)
        first_s = jnp.where(lower, block_s, got_s)
        first_r = jnp.where(lower, block_r, got_r)
        second_s = jnp.where(lower, got_s, block_s)
        block_s = first_s + jnp.exp(decay_rate * first_r) * second_s
        block_r = block_r + got_r
        bit *= 2
    return after_s


def exchange_sum(block, axis):
    size = lax.axis_size(axis)
    rows, columns = block.shape
    pieces = jnp.transpose(block.reshape(rows, size, columns // size), (1, 0, 2))
    got = lax.all_to_all(pieces, axis, 0, 0, tiled=True)
    return jnp.sum(got, axis=0)


def shards(scan_grad, step_size, scan_input, state_in, state_out, decay_rate, skip_gain):
    rows = scan_grad.shape[0]
    states = state_in.shape[1]
    in_b = jnp.broadcast_to(state_in[:, :, None], (rows, states, LANES))
    out_b = jnp.broadcast_to(state_out[:, :, None], (rows, states, LANES))
    summary, total = shard_summary(scan_grad, step_size, out_b, decay_rate)
    carried = carry_in(summary, total, decay_rate)
    scan_input_grad, b_part = shard_sweep(
        scan_grad, step_size, scan_input, in_b, out_b, decay_rate, skip_gain[None, :], carried
    )
    all_channels = scan_grad.shape[1] * lax.axis_size("exp")
    b_term = jnp.transpose(jnp.sum(b_part, axis=2)) * (1.0 / math.sqrt(all_channels))
    state_in_grad = exchange_sum(b_term, "exp")
    return (scan_input_grad, state_in_grad)


def solution(mesh):
    in_specs = (
        P("ctx", "exp"),
        P("ctx", "exp"),
        P("ctx", "exp"),
        P("ctx", None),
        P("ctx", None),
        P(None, "exp"),
        P("exp"),
    )
    out_specs = (P("ctx", "exp"), P(None, ("ctx", "exp")))
    return jax.shard_map(shards, mesh=mesh, in_specs=in_specs, out_specs=out_specs, check_vma=False)
```

```python
import math

import jax
import jax.numpy as jnp
from jax import lax
from jax.experimental import pallas as pl
from jax.experimental.pallas import tpu as pltpu
from jax.sharding import PartitionSpec as P

LANES = 128


def tiled(column_block, tiles):
    return jnp.concatenate([column_block] * tiles, axis=1)


def summary_kernel(g_ref, s_ref, outb_ref, a_ref, out_ref, gf, sf):
    rows, channels = g_ref.shape
    states = a_ref.shape[0]
    tiles = channels // LANES
    gf[...] = g_ref[...].astype(jnp.float32)
    sf[...] = s_ref[...].astype(jnp.float32)
    a = a_ref[...]

    def body(i, carry):
        incoming, decay = carry
        t = rows - 1 - i
        g_row = gf[pl.ds(t, 1), :]
        s_row = sf[pl.ds(t, 1), :]
        adjoint = tiled(outb_ref[t], tiles) * g_row + incoming
        step_decay = jnp.exp(s_row * a)
        return (step_decay * adjoint, step_decay * decay)

    start = (jnp.zeros(a.shape, jnp.float32), jnp.ones(a.shape, jnp.float32))
    summary, decay = lax.fori_loop(0, rows, body, start, unroll=8)
    out_ref[0:states, :] = summary
    out_ref[states:, :] = decay


def sweep_kernel(
    g_ref, s_ref, x_ref, inb_ref, outb_ref, a_ref, skip_ref, inc_ref,
    res_ref, bp_ref, gf, sf, wf, rf,
):
    rows, channels = g_ref.shape
    tiles = channels // LANES
    gf[...] = g_ref[...].astype(jnp.float32)
    sf[...] = s_ref[...].astype(jnp.float32)
    wf[...] = sf[...] * x_ref[...].astype(jnp.float32)
    a = a_ref[...]
    skip = skip_ref[...]

    def body(i, incoming):
        t = rows - 1 - i
        g_row = gf[pl.ds(t, 1), :]
        s_row = sf[pl.ds(t, 1), :]
        w_row = wf[pl.ds(t, 1), :]
        adjoint = tiled(outb_ref[t], tiles) * g_row + incoming
        mixed = jnp.sum(tiled(inb_ref[t], tiles) * adjoint, axis=0, keepdims=True)
        rf[pl.ds(t, 1), :] = s_row * mixed + skip * g_row
        weighted = adjoint * w_row
        part = weighted[:, 0:LANES]
        for k in range(1, tiles):
            part = part + weighted[:, k * LANES:(k + 1) * LANES]
        bp_ref[t] = part
        return jnp.exp(s_row * a) * adjoint

    lax.fori_loop(0, rows, body, inc_ref[...], unroll=8)
    res_ref[...] = rf[...].astype(res_ref.dtype)


def vmem_spec():
    return pl.BlockSpec(memory_space=pltpu.VMEM)


def shard_summary(scan_grad, step_size, out_b, decay_rate):
    rows, channels = scan_grad.shape
    states = decay_rate.shape[0]
    return pl.pallas_call(
        summary_kernel,
        out_shape=jax.ShapeDtypeStruct((2 * states, channels), jnp.float32),
        in_specs=[vmem_spec()] * 4,
        out_specs=vmem_spec(),
        scratch_shapes=[pltpu.VMEM((rows, channels), jnp.float32)] * 2,
        cost_estimate=pl.CostEstimate(
            flops=7 * rows * decay_rate.size,
            transcendentals=rows * decay_rate.size,
            bytes_accessed=4 * rows * channels + 4 * out_b.size,
        ),
    )(scan_grad, step_size, out_b, decay_rate)


def shard_sweep(scan_grad, step_size, scan_input, in_b, out_b, decay_rate, skip_gain, incoming):
    rows, channels = scan_grad.shape
    states = decay_rate.shape[0]
    return pl.pallas_call(
        sweep_kernel,
        out_shape=(
            jax.ShapeDtypeStruct((rows, channels), jnp.bfloat16),
            jax.ShapeDtypeStruct((rows, states, LANES), jnp.float32),
        ),
        in_specs=[vmem_spec()] * 8,
        out_specs=(vmem_spec(), vmem_spec()),
        scratch_shapes=[pltpu.VMEM((rows, channels), jnp.float32)] * 4,
        cost_estimate=pl.CostEstimate(
            flops=12 * rows * decay_rate.size,
            transcendentals=rows * decay_rate.size,
            bytes_accessed=8 * rows * channels + 4 * (in_b.size + out_b.size) * 2,
        ),
    )(scan_grad, step_size, scan_input, in_b, out_b, decay_rate, skip_gain, incoming)


def doubling_carry(packed, states):
    size = lax.axis_size("ctx")
    ones = jnp.concatenate([jnp.zeros_like(packed[:states]), jnp.ones_like(packed[states:])])
    packed = lax.ppermute(packed, "ctx", [(q, q - 1) for q in range(1, size)])
    packed = jnp.where(lax.axis_index("ctx") == size - 1, ones, packed)
    reach = 1
    while reach < size:
        got = lax.ppermute(packed, "ctx", [(q, q - reach) for q in range(reach, size)])
        beyond = lax.axis_index("ctx") + reach >= size
        got = jnp.where(beyond, ones, got)
        new_s = packed[:states] + packed[states:] * got[:states]
        packed = jnp.concatenate([new_s, packed[states:] * got[states:]], axis=0)
        reach *= 2
    return packed[:states]


def carry_in(packed, states):
    size = lax.axis_size("ctx")
    if size & (size - 1):
        return doubling_carry(packed, states)
    me = lax.axis_index("ctx")
    block_s, block_d = packed[:states], packed[states:]
    after_s, after_d = jnp.zeros_like(block_s), jnp.ones_like(block_d)
    bit = 1
    while bit < size:
        got = lax.ppermute(packed, "ctx", [(q, q ^ bit) for q in range(size)])
        got_s, got_d = got[:states], got[states:]
        lower = (me // bit) % 2 == 0
        after_s = jnp.where(lower, after_s + after_d * got_s, after_s)
        after_d = jnp.where(lower, after_d * got_d, after_d)
        first_s = jnp.where(lower, block_s, got_s)
        first_d = jnp.where(lower, block_d, got_d)
        second_s = jnp.where(lower, got_s, block_s)
        block_s = first_s + first_d * second_s
        block_d = block_d * got_d
        packed = jnp.concatenate([block_s, block_d], axis=0)
        bit *= 2
    return after_s


def exchange_sum(block, axis):
    size = lax.axis_size(axis)
    rows, columns = block.shape
    pieces = jnp.transpose(block.reshape(rows, size, columns // size), (1, 0, 2))
    got = lax.all_to_all(pieces, axis, 0, 0, tiled=True)
    return jnp.sum(got, axis=0)


def shards(scan_grad, step_size, scan_input, state_in, state_out, decay_rate, skip_gain):
    rows = scan_grad.shape[0]
    states = state_in.shape[1]
    in_b = jnp.broadcast_to(state_in[:, :, None], (rows, states, LANES))
    out_b = jnp.broadcast_to(state_out[:, :, None], (rows, states, LANES))
    packed = shard_summary(scan_grad, step_size, out_b, decay_rate)
    carried = carry_in(packed, states)
    scan_input_grad, b_part = shard_sweep(
        scan_grad, step_size, scan_input, in_b, out_b, decay_rate, skip_gain[None, :], carried
    )
    all_channels = scan_grad.shape[1] * lax.axis_size("exp")
    b_term = jnp.transpose(jnp.sum(b_part, axis=2)) * (1.0 / math.sqrt(all_channels))
    state_in_grad = exchange_sum(b_term, "exp")
    return (scan_input_grad, state_in_grad)


def solution(mesh):
    in_specs = (
        P("ctx", "exp"),
        P("ctx", "exp"),
        P("ctx", "exp"),
        P("ctx", None),
        P("ctx", None),
        P(None, "exp"),
        P("exp"),
    )
    out_specs = (P("ctx", "exp"), P(None, ("ctx", "exp")))
    return jax.shard_map(shards, mesh=mesh, in_specs=in_specs, out_specs=out_specs, check_vma=False)
```

```python
import math

import jax
import jax.numpy as jnp
from jax import lax
from jax.experimental import pallas as pl
from jax.experimental.pallas import tpu as pltpu
from jax.sharding import PartitionSpec as P

LANES = 128
LOG2_E = 1.4426950408889634


def tiled(column_block, tiles):
    return jnp.concatenate([column_block] * tiles, axis=1)


def summary_kernel(g_ref, s_ref, outb_ref, a_ref, out_ref, gf, sf):
    rows, channels = g_ref.shape
    states = a_ref.shape[0]
    tiles = channels // LANES
    gf[...] = g_ref[...].astype(jnp.float32)
    sf[...] = s_ref[...].astype(jnp.float32)
    out_ref[states:, :] = jnp.sum(sf[...], axis=0, keepdims=True)
    a = a_ref[...] * LOG2_E

    def body(i, incoming):
        t = rows - 1 - i
        g_row = gf[pl.ds(t, 1), :]
        s_row = sf[pl.ds(t, 1), :]
        adjoint = tiled(outb_ref[t], tiles) * g_row + incoming
        return jnp.exp2(s_row * a) * adjoint

    out_ref[0:states, :] = lax.fori_loop(
        0, rows, body, jnp.zeros(a.shape, jnp.float32), unroll=8
    )


def sweep_kernel(
    g_ref, s_ref, x_ref, inb_ref, outb_ref, a_ref, skip_ref, inc_ref,
    res_ref, bp_ref, gf, sf, wf, rf,
):
    rows, channels = g_ref.shape
    tiles = channels // LANES
    gf[...] = g_ref[...].astype(jnp.float32)
    sf[...] = s_ref[...].astype(jnp.float32)
    wf[...] = sf[...] * x_ref[...].astype(jnp.float32)
    a = a_ref[...] * LOG2_E
    skip = skip_ref[...]

    def body(i, incoming):
        t = rows - 1 - i
        g_row = gf[pl.ds(t, 1), :]
        s_row = sf[pl.ds(t, 1), :]
        w_row = wf[pl.ds(t, 1), :]
        adjoint = tiled(outb_ref[t], tiles) * g_row + incoming
        mixed = jnp.sum(tiled(inb_ref[t], tiles) * adjoint, axis=0, keepdims=True)
        rf[pl.ds(t, 1), :] = s_row * mixed + skip * g_row
        weighted = adjoint * w_row
        part = weighted[:, 0:LANES]
        for k in range(1, tiles):
            part = part + weighted[:, k * LANES:(k + 1) * LANES]
        bp_ref[t] = part
        return jnp.exp2(s_row * a) * adjoint

    lax.fori_loop(0, rows, body, inc_ref[...], unroll=8)
    res_ref[...] = rf[...].astype(res_ref.dtype)


def vmem_spec():
    return pl.BlockSpec(memory_space=pltpu.VMEM)


def shard_summary(scan_grad, step_size, out_b, decay_rate):
    rows, channels = scan_grad.shape
    states = decay_rate.shape[0]
    return pl.pallas_call(
        summary_kernel,
        out_shape=jax.ShapeDtypeStruct((states + 1, channels), jnp.float32),
        in_specs=[vmem_spec()] * 4,
        out_specs=vmem_spec(),
        scratch_shapes=[pltpu.VMEM((rows, channels), jnp.float32)] * 2,
        cost_estimate=pl.CostEstimate(
            flops=6 * rows * decay_rate.size,
            transcendentals=rows * decay_rate.size,
            bytes_accessed=4 * rows * channels + 4 * out_b.size,
        ),
    )(scan_grad, step_size, out_b, decay_rate)


def shard_sweep(scan_grad, step_size, scan_input, in_b, out_b, decay_rate, skip_gain, incoming):
    rows, channels = scan_grad.shape
    states = decay_rate.shape[0]
    return pl.pallas_call(
        sweep_kernel,
        out_shape=(
            jax.ShapeDtypeStruct((rows, channels), jnp.bfloat16),
            jax.ShapeDtypeStruct((rows, states, LANES), jnp.float32),
        ),
        in_specs=[vmem_spec()] * 8,
        out_specs=(vmem_spec(), vmem_spec()),
        scratch_shapes=[pltpu.VMEM((rows, channels), jnp.float32)] * 4,
        cost_estimate=pl.CostEstimate(
            flops=12 * rows * decay_rate.size,
            transcendentals=rows * decay_rate.size,
            bytes_accessed=8 * rows * channels + 4 * (in_b.size + out_b.size) * 2,
        ),
    )(scan_grad, step_size, scan_input, in_b, out_b, decay_rate, skip_gain, incoming)


def doubling_carry(summary, total, decay_rate):
    size = lax.axis_size("ctx")
    states = summary.shape[0]
    packed = jnp.concatenate([summary, total], axis=0)
    packed = lax.ppermute(packed, "ctx", [(q, q - 1) for q in range(1, size)])
    reach = 1
    while reach < size:
        got = lax.ppermute(packed, "ctx", [(q, q - reach) for q in range(reach, size)])
        own_s, own_r = packed[:states], packed[states:]
        new_s = own_s + jnp.exp(decay_rate * own_r) * got[:states]
        packed = jnp.concatenate([new_s, own_r + got[states:]], axis=0)
        reach *= 2
    return packed[:states]


def carry_in(packed, decay_rate):
    size = lax.axis_size("ctx")
    states = packed.shape[0] - 1
    if size & (size - 1):
        return doubling_carry(packed[:states], packed[states:], decay_rate)
    me = lax.axis_index("ctx")
    block_s, block_r = packed[:states], packed[states:]
    after_s, after_r = jnp.zeros_like(block_s), jnp.zeros_like(block_r)
    bit = 1
    while bit < size:
        if bit > 1:
            packed = jnp.concatenate([block_s, block_r], axis=0)
        got = lax.ppermute(packed, "ctx", [(q, q ^ bit) for q in range(size)])
        got_s, got_r = got[:states], got[states:]
        lower = (me // bit) % 2 == 0
        after_s = jnp.where(lower, after_s + jnp.exp(decay_rate * after_r) * got_s, after_s)
        after_r = jnp.where(lower, after_r + got_r, after_r)
        first_s = jnp.where(lower, block_s, got_s)
        first_r = jnp.where(lower, block_r, got_r)
        second_s = jnp.where(lower, got_s, block_s)
        block_s = first_s + jnp.exp(decay_rate * first_r) * second_s
        block_r = block_r + got_r
        bit *= 2
    return after_s


def exchange_sum(block, axis):
    size = lax.axis_size(axis)
    rows, columns = block.shape
    pieces = jnp.transpose(block.reshape(rows, size, columns // size), (1, 0, 2))
    got = lax.all_to_all(pieces, axis, 0, 0, tiled=True)
    return jnp.sum(got, axis=0)


def shards(scan_grad, step_size, scan_input, state_in, state_out, decay_rate, skip_gain):
    rows = scan_grad.shape[0]
    states = state_in.shape[1]
    in_b = jnp.broadcast_to(state_in[:, :, None], (rows, states, LANES))
    out_b = jnp.broadcast_to(state_out[:, :, None], (rows, states, LANES))
    packed = shard_summary(scan_grad, step_size, out_b, decay_rate)
    carried = carry_in(packed, decay_rate)
    scan_input_grad, b_part = shard_sweep(
        scan_grad, step_size, scan_input, in_b, out_b, decay_rate, skip_gain[None, :], carried
    )
    all_channels = scan_grad.shape[1] * lax.axis_size("exp")
    b_term = jnp.transpose(jnp.sum(b_part, axis=2)) * (1.0 / math.sqrt(all_channels))
    state_in_grad = exchange_sum(b_term, "exp")
    return (scan_input_grad, state_in_grad)


def solution(mesh):
    in_specs = (
        P("ctx", "exp"),
        P("ctx", "exp"),
        P("ctx", "exp"),
        P("ctx", None),
        P("ctx", None),
        P(None, "exp"),
        P("exp"),
    )
    out_specs = (P("ctx", "exp"), P(None, ("ctx", "exp")))
    return jax.shard_map(shards, mesh=mesh, in_specs=in_specs, out_specs=out_specs, check_vma=False)
```

```python
import math

import jax
import jax.numpy as jnp
from jax import lax
from jax.experimental import pallas as pl
from jax.experimental.pallas import tpu as pltpu
from jax.sharding import PartitionSpec as P

LANES = 128
LOG2_E = 1.4426950408889634


def tiled(column_block, tiles):
    return jnp.concatenate([column_block] * tiles, axis=1)


def summary_kernel(g_ref, s_ref, outb_ref, a_ref, out_ref, gf, sf):
    rows, channels = g_ref.shape
    states = a_ref.shape[0]
    tiles = channels // LANES
    gf[...] = g_ref[...].astype(jnp.float32)
    sf[...] = s_ref[...].astype(jnp.float32)
    out_ref[states:, :] = jnp.sum(sf[...], axis=0, keepdims=True)
    a = a_ref[...] * LOG2_E

    def body(i, incoming):
        t = rows - 1 - i
        g_row = gf[pl.ds(t, 1), :]
        s_row = sf[pl.ds(t, 1), :]
        adjoint = tiled(outb_ref[t], tiles) * g_row + incoming
        return jnp.exp2(s_row * a) * adjoint

    out_ref[0:states, :] = lax.fori_loop(
        0, rows, body, jnp.zeros(a.shape, jnp.float32), unroll=8
    )


def sweep_kernel(
    g_ref, s_ref, x_ref, inb_ref, outb_ref, a_ref, skip_ref, inc_ref,
    res_ref, bt_ref, gf, sf, wf, rf,
):
    rows, channels = g_ref.shape
    states = a_ref.shape[0]
    tiles = channels // LANES
    gf[...] = g_ref[...].astype(jnp.float32)
    sf[...] = s_ref[...].astype(jnp.float32)
    wf[...] = sf[...] * x_ref[...].astype(jnp.float32)
    a = a_ref[...] * LOG2_E
    skip = skip_ref[...]
    lane = lax.broadcasted_iota(jnp.int32, (states, LANES), 1)

    def run_block(base, incoming):
        def body(i, carry):
            incoming, gathered = carry
            t = base + LANES - 1 - i
            g_row = gf[pl.ds(t, 1), :]
            s_row = sf[pl.ds(t, 1), :]
            w_row = wf[pl.ds(t, 1), :]
            adjoint = tiled(outb_ref[t], tiles) * g_row + incoming
            mixed = jnp.sum(tiled(inb_ref[t], tiles) * adjoint, axis=0, keepdims=True)
            rf[pl.ds(t, 1), :] = s_row * mixed + skip * g_row
            weighted = adjoint * w_row
            part = weighted[:, 0:LANES]
            for k in range(1, tiles):
                part = part + weighted[:, k * LANES:(k + 1) * LANES]
            column = jnp.sum(part, axis=1, keepdims=True)
            gathered = jnp.where(lane == LANES - 1 - i, column, gathered)
            return (jnp.exp2(s_row * a) * adjoint, gathered)

        start = (incoming, jnp.zeros((states, LANES), jnp.float32))
        incoming, gathered = lax.fori_loop(0, LANES, body, start, unroll=8)
        bt_ref[:, base:base + LANES] = gathered
        return incoming

    incoming = inc_ref[...]
    for block in range(rows // LANES - 1, -1, -1):
        incoming = run_block(block * LANES, incoming)
    res_ref[...] = rf[...].astype(res_ref.dtype)


def vmem_spec():
    return pl.BlockSpec(memory_space=pltpu.VMEM)


def shard_summary(scan_grad, step_size, out_b, decay_rate):
    rows, channels = scan_grad.shape
    states = decay_rate.shape[0]
    return pl.pallas_call(
        summary_kernel,
        out_shape=jax.ShapeDtypeStruct((states + 1, channels), jnp.float32),
        in_specs=[vmem_spec()] * 4,
        out_specs=vmem_spec(),
        scratch_shapes=[pltpu.VMEM((rows, channels), jnp.float32)] * 2,
        cost_estimate=pl.CostEstimate(
            flops=6 * rows * decay_rate.size,
            transcendentals=rows * decay_rate.size,
            bytes_accessed=4 * rows * channels + 4 * out_b.size,
        ),
    )(scan_grad, step_size, out_b, decay_rate)


def shard_sweep(scan_grad, step_size, scan_input, in_b, out_b, decay_rate, skip_gain, incoming):
    rows, channels = scan_grad.shape
    states = decay_rate.shape[0]
    return pl.pallas_call(
        sweep_kernel,
        out_shape=(
            jax.ShapeDtypeStruct((rows, channels), jnp.bfloat16),
            jax.ShapeDtypeStruct((states, rows), jnp.float32),
        ),
        in_specs=[vmem_spec()] * 8,
        out_specs=(vmem_spec(), vmem_spec()),
        scratch_shapes=[pltpu.VMEM((rows, channels), jnp.float32)] * 4,
        cost_estimate=pl.CostEstimate(
            flops=12 * rows * decay_rate.size,
            transcendentals=rows * decay_rate.size,
            bytes_accessed=8 * rows * channels + 4 * (in_b.size + out_b.size) * 2,
        ),
    )(scan_grad, step_size, scan_input, in_b, out_b, decay_rate, skip_gain, incoming)


def doubling_carry(summary, total, decay_rate):
    size = lax.axis_size("ctx")
    states = summary.shape[0]
    packed = jnp.concatenate([summary, total], axis=0)
    packed = lax.ppermute(packed, "ctx", [(q, q - 1) for q in range(1, size)])
    reach = 1
    while reach < size:
        got = lax.ppermute(packed, "ctx", [(q, q - reach) for q in range(reach, size)])
        own_s, own_r = packed[:states], packed[states:]
        new_s = own_s + jnp.exp(decay_rate * own_r) * got[:states]
        packed = jnp.concatenate([new_s, own_r + got[states:]], axis=0)
        reach *= 2
    return packed[:states]


def carry_in(packed, decay_rate):
    size = lax.axis_size("ctx")
    states = packed.shape[0] - 1
    if size & (size - 1):
        return doubling_carry(packed[:states], packed[states:], decay_rate)
    me = lax.axis_index("ctx")
    block_s, block_r = packed[:states], packed[states:]
    after_s, after_r = jnp.zeros_like(block_s), jnp.zeros_like(block_r)
    bit = 1
    while bit < size:
        if bit > 1:
            packed = jnp.concatenate([block_s, block_r], axis=0)
        got = lax.ppermute(packed, "ctx", [(q, q ^ bit) for q in range(size)])
        got_s, got_r = got[:states], got[states:]
        lower = (me // bit) % 2 == 0
        after_s = jnp.where(lower, after_s + jnp.exp(decay_rate * after_r) * got_s, after_s)
        after_r = jnp.where(lower, after_r + got_r, after_r)
        first_s = jnp.where(lower, block_s, got_s)
        first_r = jnp.where(lower, block_r, got_r)
        second_s = jnp.where(lower, got_s, block_s)
        block_s = first_s + jnp.exp(decay_rate * first_r) * second_s
        block_r = block_r + got_r
        bit *= 2
    return after_s


def exchange_sum(block, axis):
    size = lax.axis_size(axis)
    rows, columns = block.shape
    pieces = jnp.transpose(block.reshape(rows, size, columns // size), (1, 0, 2))
    got = lax.all_to_all(pieces, axis, 0, 0, tiled=True)
    return jnp.sum(got, axis=0)


def shards(scan_grad, step_size, scan_input, state_in, state_out, decay_rate, skip_gain):
    rows = scan_grad.shape[0]
    states = state_in.shape[1]
    in_b = jnp.broadcast_to(state_in[:, :, None], (rows, states, LANES))
    out_b = jnp.broadcast_to(state_out[:, :, None], (rows, states, LANES))
    packed = shard_summary(scan_grad, step_size, out_b, decay_rate)
    carried = carry_in(packed, decay_rate)
    scan_input_grad, b_t = shard_sweep(
        scan_grad, step_size, scan_input, in_b, out_b, decay_rate, skip_gain[None, :], carried
    )
    all_channels = scan_grad.shape[1] * lax.axis_size("exp")
    b_term = b_t * (1.0 / math.sqrt(all_channels))
    state_in_grad = exchange_sum(b_term, "exp")
    return (scan_input_grad, state_in_grad)


def solution(mesh):
    in_specs = (
        P("ctx", "exp"),
        P("ctx", "exp"),
        P("ctx", "exp"),
        P("ctx", None),
        P("ctx", None),
        P(None, "exp"),
        P("exp"),
    )
    out_specs = (P("ctx", "exp"), P(None, ("ctx", "exp")))
    return jax.shard_map(shards, mesh=mesh, in_specs=in_specs, out_specs=out_specs, check_vma=False)
```

```python
import math

import jax
import jax.numpy as jnp
from jax import lax
from jax.experimental import pallas as pl
from jax.experimental.pallas import tpu as pltpu
from jax.sharding import PartitionSpec as P

LANES = 128
LOG2_E = 1.4426950408889634


def tiled(column_block, tiles):
    return jnp.concatenate([column_block] * tiles, axis=1)


def lane_column(block, j, channels):
    lane = lax.broadcasted_iota(jnp.int32, block.shape, 1)
    column = jnp.sum(jnp.where(lane == j, block, 0.0), axis=1, keepdims=True)
    return jnp.broadcast_to(column, (block.shape[0], channels))


def summary_kernel(g_ref, s_ref, outt_ref, a_ref, out_ref, gf, sf):
    rows, channels = g_ref.shape
    states = a_ref.shape[0]
    gf[...] = g_ref[...].astype(jnp.float32)
    sf[...] = s_ref[...].astype(jnp.float32)
    out_ref[states:, :] = jnp.sum(sf[...], axis=0, keepdims=True)
    a = a_ref[...] * LOG2_E

    def run_block(base, incoming):
        out_block = outt_ref[:, base:base + LANES]

        def body(i, incoming):
            j = LANES - 1 - i
            t = base + j
            g_row = gf[pl.ds(t, 1), :]
            s_row = sf[pl.ds(t, 1), :]
            adjoint = lane_column(out_block, j, channels) * g_row + incoming
            return jnp.exp2(s_row * a) * adjoint

        return lax.fori_loop(0, LANES, body, incoming, unroll=8)

    incoming = jnp.zeros(a.shape, jnp.float32)
    for block in range(rows // LANES - 1, -1, -1):
        incoming = run_block(block * LANES, incoming)
    out_ref[0:states, :] = incoming


def sweep_kernel(
    g_ref, s_ref, x_ref, int_ref, outt_ref, a_ref, skip_ref, inc_ref,
    res_ref, bt_ref, gf, sf, wf, rf,
):
    rows, channels = g_ref.shape
    states = a_ref.shape[0]
    tiles = channels // LANES
    gf[...] = g_ref[...].astype(jnp.float32)
    sf[...] = s_ref[...].astype(jnp.float32)
    wf[...] = sf[...] * x_ref[...].astype(jnp.float32)
    a = a_ref[...] * LOG2_E
    skip = skip_ref[...]
    lane = lax.broadcasted_iota(jnp.int32, (states, LANES), 1)

    def run_block(base, incoming):
        in_block = int_ref[:, base:base + LANES]
        out_block = outt_ref[:, base:base + LANES]

        def body(i, carry):
            incoming, gathered = carry
            j = LANES - 1 - i
            t = base + j
            g_row = gf[pl.ds(t, 1), :]
            s_row = sf[pl.ds(t, 1), :]
            w_row = wf[pl.ds(t, 1), :]
            adjoint = lane_column(out_block, j, channels) * g_row + incoming
            mixed = jnp.sum(lane_column(in_block, j, channels) * adjoint, axis=0, keepdims=True)
            rf[pl.ds(t, 1), :] = s_row * mixed + skip * g_row
            weighted = adjoint * w_row
            part = weighted[:, 0:LANES]
            for k in range(1, tiles):
                part = part + weighted[:, k * LANES:(k + 1) * LANES]
            column = jnp.sum(part, axis=1, keepdims=True)
            gathered = jnp.where(lane == j, column, gathered)
            return (jnp.exp2(s_row * a) * adjoint, gathered)

        start = (incoming, jnp.zeros((states, LANES), jnp.float32))
        incoming, gathered = lax.fori_loop(0, LANES, body, start, unroll=8)
        bt_ref[:, base:base + LANES] = gathered
        return incoming

    incoming = inc_ref[...]
    for block in range(rows // LANES - 1, -1, -1):
        incoming = run_block(block * LANES, incoming)
    res_ref[...] = rf[...].astype(res_ref.dtype)


def vmem_spec():
    return pl.BlockSpec(memory_space=pltpu.VMEM)


def shard_summary(scan_grad, step_size, out_b, decay_rate):
    rows, channels = scan_grad.shape
    states = decay_rate.shape[0]
    return pl.pallas_call(
        summary_kernel,
        out_shape=jax.ShapeDtypeStruct((states + 1, channels), jnp.float32),
        in_specs=[vmem_spec()] * 4,
        out_specs=vmem_spec(),
        scratch_shapes=[pltpu.VMEM((rows, channels), jnp.float32)] * 2,
        cost_estimate=pl.CostEstimate(
            flops=6 * rows * decay_rate.size,
            transcendentals=rows * decay_rate.size,
            bytes_accessed=4 * rows * channels + 4 * out_b.size,
        ),
    )(scan_grad, step_size, out_b, decay_rate)


def shard_sweep(scan_grad, step_size, scan_input, in_b, out_b, decay_rate, skip_gain, incoming):
    rows, channels = scan_grad.shape
    states = decay_rate.shape[0]
    return pl.pallas_call(
        sweep_kernel,
        out_shape=(
            jax.ShapeDtypeStruct((rows, channels), jnp.bfloat16),
            jax.ShapeDtypeStruct((states, rows), jnp.float32),
        ),
        in_specs=[vmem_spec()] * 8,
        out_specs=(vmem_spec(), vmem_spec()),
        scratch_shapes=[pltpu.VMEM((rows, channels), jnp.float32)] * 4,
        cost_estimate=pl.CostEstimate(
            flops=12 * rows * decay_rate.size,
            transcendentals=rows * decay_rate.size,
            bytes_accessed=8 * rows * channels + 4 * (in_b.size + out_b.size) * 2,
        ),
    )(scan_grad, step_size, scan_input, in_b, out_b, decay_rate, skip_gain, incoming)


def doubling_carry(summary, total, decay_rate):
    size = lax.axis_size("ctx")
    states = summary.shape[0]
    packed = jnp.concatenate([summary, total], axis=0)
    packed = lax.ppermute(packed, "ctx", [(q, q - 1) for q in range(1, size)])
    reach = 1
    while reach < size:
        got = lax.ppermute(packed, "ctx", [(q, q - reach) for q in range(reach, size)])
        own_s, own_r = packed[:states], packed[states:]
        new_s = own_s + jnp.exp(decay_rate * own_r) * got[:states]
        packed = jnp.concatenate([new_s, own_r + got[states:]], axis=0)
        reach *= 2
    return packed[:states]


def carry_in(packed, decay_rate):
    size = lax.axis_size("ctx")
    states = packed.shape[0] - 1
    if size & (size - 1):
        return doubling_carry(packed[:states], packed[states:], decay_rate)
    me = lax.axis_index("ctx")
    block_s, block_r = packed[:states], packed[states:]
    after_s, after_r = jnp.zeros_like(block_s), jnp.zeros_like(block_r)
    bit = 1
    while bit < size:
        if bit > 1:
            packed = jnp.concatenate([block_s, block_r], axis=0)
        got = lax.ppermute(packed, "ctx", [(q, q ^ bit) for q in range(size)])
        got_s, got_r = got[:states], got[states:]
        lower = (me // bit) % 2 == 0
        after_s = jnp.where(lower, after_s + jnp.exp(decay_rate * after_r) * got_s, after_s)
        after_r = jnp.where(lower, after_r + got_r, after_r)
        first_s = jnp.where(lower, block_s, got_s)
        first_r = jnp.where(lower, block_r, got_r)
        second_s = jnp.where(lower, got_s, block_s)
        block_s = first_s + jnp.exp(decay_rate * first_r) * second_s
        block_r = block_r + got_r
        bit *= 2
    return after_s


def exchange_sum(block, axis):
    size = lax.axis_size(axis)
    rows, columns = block.shape
    pieces = jnp.transpose(block.reshape(rows, size, columns // size), (1, 0, 2))
    got = lax.all_to_all(pieces, axis, 0, 0, tiled=True)
    return jnp.sum(got, axis=0)


def shards(scan_grad, step_size, scan_input, state_in, state_out, decay_rate, skip_gain):
    rows = scan_grad.shape[0]
    states = state_in.shape[1]
    in_b = jnp.transpose(state_in)
    out_b = jnp.transpose(state_out)
    packed = shard_summary(scan_grad, step_size, out_b, decay_rate)
    carried = carry_in(packed, decay_rate)
    scan_input_grad, b_t = shard_sweep(
        scan_grad, step_size, scan_input, in_b, out_b, decay_rate, skip_gain[None, :], carried
    )
    all_channels = scan_grad.shape[1] * lax.axis_size("exp")
    b_term = b_t * (1.0 / math.sqrt(all_channels))
    state_in_grad = exchange_sum(b_term, "exp")
    return (scan_input_grad, state_in_grad)


def solution(mesh):
    in_specs = (
        P("ctx", "exp"),
        P("ctx", "exp"),
        P("ctx", "exp"),
        P("ctx", None),
        P("ctx", None),
        P(None, "exp"),
        P("exp"),
    )
    out_specs = (P("ctx", "exp"), P(None, ("ctx", "exp")))
    return jax.shard_map(shards, mesh=mesh, in_specs=in_specs, out_specs=out_specs, check_vma=False)
```

```python
import math

import jax
import jax.numpy as jnp
from jax import lax
from jax.experimental import pallas as pl
from jax.experimental.pallas import tpu as pltpu
from jax.sharding import PartitionSpec as P

LANES = 128
LOG2_E = 1.4426950408889634


def tiled(column_block, tiles):
    return jnp.concatenate([column_block] * tiles, axis=1)


def lane_column(block, j, channels):
    lane = lax.broadcasted_iota(jnp.int32, block.shape, 1)
    column = jnp.sum(jnp.where(lane == j, block, 0.0), axis=1, keepdims=True)
    return jnp.broadcast_to(column, (block.shape[0], channels))


def summary_kernel(g_ref, s_ref, outt_ref, a_ref, out_ref, gf, sf):
    rows, channels = g_ref.shape
    states = a_ref.shape[0]
    gf[...] = g_ref[...].astype(jnp.float32)
    sf[...] = s_ref[...].astype(jnp.float32)
    out_ref[states:, :] = jnp.sum(sf[...], axis=0, keepdims=True)
    a = a_ref[...] * LOG2_E

    def run_block(base, incoming):
        out_block = outt_ref[:, base:base + LANES]

        def body(i, incoming):
            j = LANES - 1 - i
            t = base + j
            g_row = gf[pl.ds(t, 1), :]
            s_row = sf[pl.ds(t, 1), :]
            adjoint = lane_column(out_block, j, channels) * g_row + incoming
            return jnp.exp2(s_row * a) * adjoint

        return lax.fori_loop(0, LANES, body, incoming, unroll=16)

    incoming = jnp.zeros(a.shape, jnp.float32)
    for block in range(rows // LANES - 1, -1, -1):
        incoming = run_block(block * LANES, incoming)
    out_ref[0:states, :] = incoming


def sweep_kernel(
    g_ref, s_ref, x_ref, int_ref, outt_ref, a_ref, skip_ref, inc_ref,
    res_ref, bt_ref, gf, sf, wf, rf,
):
    rows, channels = g_ref.shape
    states = a_ref.shape[0]
    tiles = channels // LANES
    gf[...] = g_ref[...].astype(jnp.float32)
    sf[...] = s_ref[...].astype(jnp.float32)
    wf[...] = sf[...] * x_ref[...].astype(jnp.float32)
    a = a_ref[...] * LOG2_E
    skip = skip_ref[...]
    lane = lax.broadcasted_iota(jnp.int32, (states, LANES), 1)

    def run_block(base, incoming):
        in_block = int_ref[:, base:base + LANES]
        out_block = outt_ref[:, base:base + LANES]

        def body(i, carry):
            incoming, gathered = carry
            j = LANES - 1 - i
            t = base + j
            g_row = gf[pl.ds(t, 1), :]
            s_row = sf[pl.ds(t, 1), :]
            w_row = wf[pl.ds(t, 1), :]
            adjoint = lane_column(out_block, j, channels) * g_row + incoming
            mixed = jnp.sum(lane_column(in_block, j, channels) * adjoint, axis=0, keepdims=True)
            rf[pl.ds(t, 1), :] = s_row * mixed + skip * g_row
            weighted = adjoint * w_row
            part = weighted[:, 0:LANES]
            for k in range(1, tiles):
                part = part + weighted[:, k * LANES:(k + 1) * LANES]
            column = jnp.sum(part, axis=1, keepdims=True)
            gathered = jnp.where(lane == j, column, gathered)
            return (jnp.exp2(s_row * a) * adjoint, gathered)

        start = (incoming, jnp.zeros((states, LANES), jnp.float32))
        incoming, gathered = lax.fori_loop(0, LANES, body, start, unroll=16)
        bt_ref[:, base:base + LANES] = gathered
        return incoming

    incoming = inc_ref[...]
    for block in range(rows // LANES - 1, -1, -1):
        incoming = run_block(block * LANES, incoming)
    res_ref[...] = rf[...].astype(res_ref.dtype)


def vmem_spec():
    return pl.BlockSpec(memory_space=pltpu.VMEM)


def shard_summary(scan_grad, step_size, out_b, decay_rate):
    rows, channels = scan_grad.shape
    states = decay_rate.shape[0]
    return pl.pallas_call(
        summary_kernel,
        out_shape=jax.ShapeDtypeStruct((states + 1, channels), jnp.float32),
        in_specs=[vmem_spec()] * 4,
        out_specs=vmem_spec(),
        scratch_shapes=[pltpu.VMEM((rows, channels), jnp.float32)] * 2,
        cost_estimate=pl.CostEstimate(
            flops=6 * rows * decay_rate.size,
            transcendentals=rows * decay_rate.size,
            bytes_accessed=4 * rows * channels + 4 * out_b.size,
        ),
    )(scan_grad, step_size, out_b, decay_rate)


def shard_sweep(scan_grad, step_size, scan_input, in_b, out_b, decay_rate, skip_gain, incoming):
    rows, channels = scan_grad.shape
    states = decay_rate.shape[0]
    return pl.pallas_call(
        sweep_kernel,
        out_shape=(
            jax.ShapeDtypeStruct((rows, channels), jnp.bfloat16),
            jax.ShapeDtypeStruct((states, rows), jnp.float32),
        ),
        in_specs=[vmem_spec()] * 8,
        out_specs=(vmem_spec(), vmem_spec()),
        scratch_shapes=[pltpu.VMEM((rows, channels), jnp.float32)] * 4,
        cost_estimate=pl.CostEstimate(
            flops=12 * rows * decay_rate.size,
            transcendentals=rows * decay_rate.size,
            bytes_accessed=8 * rows * channels + 4 * (in_b.size + out_b.size) * 2,
        ),
    )(scan_grad, step_size, scan_input, in_b, out_b, decay_rate, skip_gain, incoming)


def doubling_carry(summary, total, decay_rate):
    size = lax.axis_size("ctx")
    states = summary.shape[0]
    packed = jnp.concatenate([summary, total], axis=0)
    packed = lax.ppermute(packed, "ctx", [(q, q - 1) for q in range(1, size)])
    reach = 1
    while reach < size:
        got = lax.ppermute(packed, "ctx", [(q, q - reach) for q in range(reach, size)])
        own_s, own_r = packed[:states], packed[states:]
        new_s = own_s + jnp.exp(decay_rate * own_r) * got[:states]
        packed = jnp.concatenate([new_s, own_r + got[states:]], axis=0)
        reach *= 2
    return packed[:states]


def carry_in(packed, decay_rate):
    size = lax.axis_size("ctx")
    states = packed.shape[0] - 1
    if size & (size - 1):
        return doubling_carry(packed[:states], packed[states:], decay_rate)
    me = lax.axis_index("ctx")
    block_s, block_r = packed[:states], packed[states:]
    after_s, after_r = jnp.zeros_like(block_s), jnp.zeros_like(block_r)
    bit = 1
    while bit < size:
        if bit > 1:
            packed = jnp.concatenate([block_s, block_r], axis=0)
        got = lax.ppermute(packed, "ctx", [(q, q ^ bit) for q in range(size)])
        got_s, got_r = got[:states], got[states:]
        lower = (me // bit) % 2 == 0
        after_s = jnp.where(lower, after_s + jnp.exp(decay_rate * after_r) * got_s, after_s)
        after_r = jnp.where(lower, after_r + got_r, after_r)
        first_s = jnp.where(lower, block_s, got_s)
        first_r = jnp.where(lower, block_r, got_r)
        second_s = jnp.where(lower, got_s, block_s)
        block_s = first_s + jnp.exp(decay_rate * first_r) * second_s
        block_r = block_r + got_r
        bit *= 2
    return after_s


def exchange_sum(block, axis):
    size = lax.axis_size(axis)
    rows, columns = block.shape
    pieces = jnp.transpose(block.reshape(rows, size, columns // size), (1, 0, 2))
    got = lax.all_to_all(pieces, axis, 0, 0, tiled=True)
    return jnp.sum(got, axis=0)


def shards(scan_grad, step_size, scan_input, state_in, state_out, decay_rate, skip_gain):
    rows = scan_grad.shape[0]
    states = state_in.shape[1]
    in_b = jnp.transpose(state_in)
    out_b = jnp.transpose(state_out)
    packed = shard_summary(scan_grad, step_size, out_b, decay_rate)
    carried = carry_in(packed, decay_rate)
    scan_input_grad, b_t = shard_sweep(
        scan_grad, step_size, scan_input, in_b, out_b, decay_rate, skip_gain[None, :], carried
    )
    all_channels = scan_grad.shape[1] * lax.axis_size("exp")
    b_term = b_t * (1.0 / math.sqrt(all_channels))
    state_in_grad = exchange_sum(b_term, "exp")
    return (scan_input_grad, state_in_grad)


def solution(mesh):
    in_specs = (
        P("ctx", "exp"),
        P("ctx", "exp"),
        P("ctx", "exp"),
        P("ctx", None),
        P("ctx", None),
        P(None, "exp"),
        P("exp"),
    )
    out_specs = (P("ctx", "exp"), P(None, ("ctx", "exp")))
    return jax.shard_map(shards, mesh=mesh, in_specs=in_specs, out_specs=out_specs, check_vma=False)
```

```python
import math

import jax
import jax.numpy as jnp
from jax import lax
from jax.experimental import pallas as pl
from jax.experimental.pallas import tpu as pltpu
from jax.sharding import PartitionSpec as P

LANES = 128
LOG2_E = 1.4426950408889634


def tiled(column_block, tiles):
    return jnp.concatenate([column_block] * tiles, axis=1)


def lane_column(block, j, channels):
    lane = lax.broadcasted_iota(jnp.int32, block.shape, 1)
    column = jnp.sum(jnp.where(lane == j, block, 0.0), axis=1, keepdims=True)
    return jnp.broadcast_to(column, (block.shape[0], channels))


def summary_kernel(g_ref, s_ref, outt_ref, a_ref, out_ref, gf, sf):
    rows, channels = g_ref.shape
    states = a_ref.shape[0]
    gf[...] = g_ref[...].astype(jnp.float32)
    sf[...] = s_ref[...].astype(jnp.float32)
    out_ref[states:, :] = jnp.sum(sf[...], axis=0, keepdims=True)
    a = a_ref[...] * LOG2_E

    def run_block(base, incoming):
        out_block = outt_ref[:, base:base + LANES]

        def body(i, incoming):
            j = LANES - 1 - i
            t = base + j
            g_row = gf[pl.ds(t, 1), :]
            s_row = sf[pl.ds(t, 1), :]
            adjoint = lane_column(out_block, j, channels) * g_row + incoming
            return jnp.exp2(s_row * a) * adjoint

        return lax.fori_loop(0, LANES, body, incoming, unroll=32)

    incoming = jnp.zeros(a.shape, jnp.float32)
    for block in range(rows // LANES - 1, -1, -1):
        incoming = run_block(block * LANES, incoming)
    out_ref[0:states, :] = incoming


def sweep_kernel(
    g_ref, s_ref, x_ref, int_ref, outt_ref, a_ref, skip_ref, inc_ref,
    res_ref, bt_ref, gf, sf, wf, rf,
):
    rows, channels = g_ref.shape
    states = a_ref.shape[0]
    tiles = channels // LANES
    gf[...] = g_ref[...].astype(jnp.float32)
    sf[...] = s_ref[...].astype(jnp.float32)
    wf[...] = sf[...] * x_ref[...].astype(jnp.float32)
    a = a_ref[...] * LOG2_E
    skip = skip_ref[...]
    lane = lax.broadcasted_iota(jnp.int32, (states, LANES), 1)

    def run_block(base, incoming):
        in_block = int_ref[:, base:base + LANES]
        out_block = outt_ref[:, base:base + LANES]

        def body(i, carry):
            incoming, gathered = carry
            j = LANES - 1 - i
            t = base + j
            g_row = gf[pl.ds(t, 1), :]
            s_row = sf[pl.ds(t, 1), :]
            w_row = wf[pl.ds(t, 1), :]
            adjoint = lane_column(out_block, j, channels) * g_row + incoming
            mixed = jnp.sum(lane_column(in_block, j, channels) * adjoint, axis=0, keepdims=True)
            rf[pl.ds(t, 1), :] = s_row * mixed + skip * g_row
            weighted = adjoint * w_row
            part = weighted[:, 0:LANES]
            for k in range(1, tiles):
                part = part + weighted[:, k * LANES:(k + 1) * LANES]
            column = jnp.sum(part, axis=1, keepdims=True)
            gathered = jnp.where(lane == j, column, gathered)
            return (jnp.exp2(s_row * a) * adjoint, gathered)

        start = (incoming, jnp.zeros((states, LANES), jnp.float32))
        incoming, gathered = lax.fori_loop(0, LANES, body, start, unroll=32)
        bt_ref[:, base:base + LANES] = gathered
        return incoming

    incoming = inc_ref[...]
    for block in range(rows // LANES - 1, -1, -1):
        incoming = run_block(block * LANES, incoming)
    res_ref[...] = rf[...].astype(res_ref.dtype)


def vmem_spec():
    return pl.BlockSpec(memory_space=pltpu.VMEM)


def shard_summary(scan_grad, step_size, out_b, decay_rate):
    rows, channels = scan_grad.shape
    states = decay_rate.shape[0]
    return pl.pallas_call(
        summary_kernel,
        out_shape=jax.ShapeDtypeStruct((states + 1, channels), jnp.float32),
        in_specs=[vmem_spec()] * 4,
        out_specs=vmem_spec(),
        scratch_shapes=[pltpu.VMEM((rows, channels), jnp.float32)] * 2,
        cost_estimate=pl.CostEstimate(
            flops=6 * rows * decay_rate.size,
            transcendentals=rows * decay_rate.size,
            bytes_accessed=4 * rows * channels + 4 * out_b.size,
        ),
    )(scan_grad, step_size, out_b, decay_rate)


def shard_sweep(scan_grad, step_size, scan_input, in_b, out_b, decay_rate, skip_gain, incoming):
    rows, channels = scan_grad.shape
    states = decay_rate.shape[0]
    return pl.pallas_call(
        sweep_kernel,
        out_shape=(
            jax.ShapeDtypeStruct((rows, channels), jnp.bfloat16),
            jax.ShapeDtypeStruct((states, rows), jnp.float32),
        ),
        in_specs=[vmem_spec()] * 8,
        out_specs=(vmem_spec(), vmem_spec()),
        scratch_shapes=[pltpu.VMEM((rows, channels), jnp.float32)] * 4,
        cost_estimate=pl.CostEstimate(
            flops=12 * rows * decay_rate.size,
            transcendentals=rows * decay_rate.size,
            bytes_accessed=8 * rows * channels + 4 * (in_b.size + out_b.size) * 2,
        ),
    )(scan_grad, step_size, scan_input, in_b, out_b, decay_rate, skip_gain, incoming)


def doubling_carry(summary, total, decay_rate):
    size = lax.axis_size("ctx")
    states = summary.shape[0]
    packed = jnp.concatenate([summary, total], axis=0)
    packed = lax.ppermute(packed, "ctx", [(q, q - 1) for q in range(1, size)])
    reach = 1
    while reach < size:
        got = lax.ppermute(packed, "ctx", [(q, q - reach) for q in range(reach, size)])
        own_s, own_r = packed[:states], packed[states:]
        new_s = own_s + jnp.exp(decay_rate * own_r) * got[:states]
        packed = jnp.concatenate([new_s, own_r + got[states:]], axis=0)
        reach *= 2
    return packed[:states]


def carry_in(packed, decay_rate):
    size = lax.axis_size("ctx")
    states = packed.shape[0] - 1
    if size & (size - 1):
        return doubling_carry(packed[:states], packed[states:], decay_rate)
    me = lax.axis_index("ctx")
    block_s, block_r = packed[:states], packed[states:]
    after_s, after_r = jnp.zeros_like(block_s), jnp.zeros_like(block_r)
    bit = 1
    while bit < size:
        if bit > 1:
            packed = jnp.concatenate([block_s, block_r], axis=0)
        got = lax.ppermute(packed, "ctx", [(q, q ^ bit) for q in range(size)])
        got_s, got_r = got[:states], got[states:]
        lower = (me // bit) % 2 == 0
        after_s = jnp.where(lower, after_s + jnp.exp(decay_rate * after_r) * got_s, after_s)
        after_r = jnp.where(lower, after_r + got_r, after_r)
        first_s = jnp.where(lower, block_s, got_s)
        first_r = jnp.where(lower, block_r, got_r)
        second_s = jnp.where(lower, got_s, block_s)
        block_s = first_s + jnp.exp(decay_rate * first_r) * second_s
        block_r = block_r + got_r
        bit *= 2
    return after_s


def exchange_sum(block, axis):
    size = lax.axis_size(axis)
    rows, columns = block.shape
    pieces = jnp.transpose(block.reshape(rows, size, columns // size), (1, 0, 2))
    got = lax.all_to_all(pieces, axis, 0, 0, tiled=True)
    return jnp.sum(got, axis=0)


def shards(scan_grad, step_size, scan_input, state_in, state_out, decay_rate, skip_gain):
    rows = scan_grad.shape[0]
    states = state_in.shape[1]
    in_b = jnp.transpose(state_in)
    out_b = jnp.transpose(state_out)
    packed = shard_summary(scan_grad, step_size, out_b, decay_rate)
    carried = carry_in(packed, decay_rate)
    scan_input_grad, b_t = shard_sweep(
        scan_grad, step_size, scan_input, in_b, out_b, decay_rate, skip_gain[None, :], carried
    )
    all_channels = scan_grad.shape[1] * lax.axis_size("exp")
    b_term = b_t * (1.0 / math.sqrt(all_channels))
    state_in_grad = exchange_sum(b_term, "exp")
    return (scan_input_grad, state_in_grad)


def solution(mesh):
    in_specs = (
        P("ctx", "exp"),
        P("ctx", "exp"),
        P("ctx", "exp"),
        P("ctx", None),
        P("ctx", None),
        P(None, "exp"),
        P("exp"),
    )
    out_specs = (P("ctx", "exp"), P(None, ("ctx", "exp")))
    return jax.shard_map(shards, mesh=mesh, in_specs=in_specs, out_specs=out_specs, check_vma=False)
```

```python
import functools
import math

import jax
import jax.numpy as jnp
from jax import lax
from jax.experimental import pallas as pl
from jax.experimental.pallas import tpu as pltpu
from jax.sharding import PartitionSpec as P

LANES = 128
LOG2_E = 1.4426950408889634


def tiled(column_block, tiles):
    return jnp.concatenate([column_block] * tiles, axis=1)


def lane_column(block, j, channels):
    lane = lax.broadcasted_iota(jnp.int32, block.shape, 1)
    column = jnp.sum(jnp.where(lane == j, block, 0.0), axis=1, keepdims=True)
    return jnp.broadcast_to(column, (block.shape[0], channels))


def summary_kernel(g_ref, s_ref, outt_ref, a_ref, out_ref, gf, sf):
    rows, channels = g_ref.shape
    states = a_ref.shape[0]
    gf[...] = g_ref[...].astype(jnp.float32)
    sf[...] = s_ref[...].astype(jnp.float32)
    out_ref[states:, :] = jnp.sum(sf[...], axis=0, keepdims=True)
    a = a_ref[...] * LOG2_E

    def run_block(base, incoming):
        out_block = outt_ref[:, base:base + LANES]

        def body(i, incoming):
            j = LANES - 1 - i
            t = base + j
            g_row = gf[pl.ds(t, 1), :]
            s_row = sf[pl.ds(t, 1), :]
            adjoint = lane_column(out_block, j, channels) * g_row + incoming
            return jnp.exp2(s_row * a) * adjoint

        return lax.fori_loop(0, LANES, body, incoming, unroll=32)

    incoming = jnp.zeros(a.shape, jnp.float32)
    for block in range(rows // LANES - 1, -1, -1):
        incoming = run_block(block * LANES, incoming)
    out_ref[0:states, :] = incoming


def sweep_kernel(
    g_ref, s_ref, x_ref, int_ref, outt_ref, a_ref, skip_ref, inc_ref,
    res_ref, bt_ref, gf, sf, wf, rf, *, scale,
):
    rows, channels = g_ref.shape
    states = a_ref.shape[0]
    tiles = channels // LANES
    gf[...] = g_ref[...].astype(jnp.float32)
    sf[...] = s_ref[...].astype(jnp.float32)
    wf[...] = sf[...] * x_ref[...].astype(jnp.float32)
    a = a_ref[...] * LOG2_E
    skip = skip_ref[...]
    lane = lax.broadcasted_iota(jnp.int32, (states, LANES), 1)

    def run_block(base, incoming):
        in_block = int_ref[:, base:base + LANES]
        out_block = outt_ref[:, base:base + LANES]

        def body(i, carry):
            incoming, gathered = carry
            j = LANES - 1 - i
            t = base + j
            g_row = gf[pl.ds(t, 1), :]
            s_row = sf[pl.ds(t, 1), :]
            w_row = wf[pl.ds(t, 1), :]
            adjoint = lane_column(out_block, j, channels) * g_row + incoming
            mixed = jnp.sum(lane_column(in_block, j, channels) * adjoint, axis=0, keepdims=True)
            rf[pl.ds(t, 1), :] = s_row * mixed + skip * g_row
            weighted = adjoint * w_row
            part = weighted[:, 0:LANES]
            for k in range(1, tiles):
                part = part + weighted[:, k * LANES:(k + 1) * LANES]
            column = jnp.sum(part, axis=1, keepdims=True)
            gathered = jnp.where(lane == j, column, gathered)
            return (jnp.exp2(s_row * a) * adjoint, gathered)

        start = (incoming, jnp.zeros((states, LANES), jnp.float32))
        incoming, gathered = lax.fori_loop(0, LANES, body, start, unroll=32)
        bt_ref[:, base:base + LANES] = gathered * scale
        return incoming

    incoming = inc_ref[...]
    for block in range(rows // LANES - 1, -1, -1):
        incoming = run_block(block * LANES, incoming)
    res_ref[...] = rf[...].astype(res_ref.dtype)


def vmem_spec():
    return pl.BlockSpec(memory_space=pltpu.VMEM)


def shard_summary(scan_grad, step_size, out_b, decay_rate):
    rows, channels = scan_grad.shape
    states = decay_rate.shape[0]
    return pl.pallas_call(
        summary_kernel,
        out_shape=jax.ShapeDtypeStruct((states + 1, channels), jnp.float32),
        in_specs=[vmem_spec()] * 4,
        out_specs=vmem_spec(),
        scratch_shapes=[pltpu.VMEM((rows, channels), jnp.float32)] * 2,
        cost_estimate=pl.CostEstimate(
            flops=6 * rows * decay_rate.size,
            transcendentals=rows * decay_rate.size,
            bytes_accessed=4 * rows * channels + 4 * out_b.size,
        ),
    )(scan_grad, step_size, out_b, decay_rate)


def shard_sweep(scan_grad, step_size, scan_input, in_b, out_b, decay_rate, skip_gain, incoming, scale):
    rows, channels = scan_grad.shape
    states = decay_rate.shape[0]
    return pl.pallas_call(
        functools.partial(sweep_kernel, scale=scale),
        out_shape=(
            jax.ShapeDtypeStruct((rows, channels), jnp.bfloat16),
            jax.ShapeDtypeStruct((states, rows), jnp.float32),
        ),
        in_specs=[vmem_spec()] * 8,
        out_specs=(vmem_spec(), vmem_spec()),
        scratch_shapes=[pltpu.VMEM((rows, channels), jnp.float32)] * 4,
        cost_estimate=pl.CostEstimate(
            flops=12 * rows * decay_rate.size,
            transcendentals=rows * decay_rate.size,
            bytes_accessed=8 * rows * channels + 4 * (in_b.size + out_b.size) * 2,
        ),
    )(scan_grad, step_size, scan_input, in_b, out_b, decay_rate, skip_gain, incoming)


def doubling_carry(summary, total, decay_rate):
    size = lax.axis_size("ctx")
    states = summary.shape[0]
    packed = jnp.concatenate([summary, total], axis=0)
    packed = lax.ppermute(packed, "ctx", [(q, q - 1) for q in range(1, size)])
    reach = 1
    while reach < size:
        got = lax.ppermute(packed, "ctx", [(q, q - reach) for q in range(reach, size)])
        own_s, own_r = packed[:states], packed[states:]
        new_s = own_s + jnp.exp(decay_rate * own_r) * got[:states]
        packed = jnp.concatenate([new_s, own_r + got[states:]], axis=0)
        reach *= 2
    return packed[:states]


def carry_in(packed, decay_rate):
    size = lax.axis_size("ctx")
    states = packed.shape[0] - 1
    if size & (size - 1):
        return doubling_carry(packed[:states], packed[states:], decay_rate)
    me = lax.axis_index("ctx")
    block_s, block_r = packed[:states], packed[states:]
    after_s, after_r = jnp.zeros_like(block_s), jnp.zeros_like(block_r)
    bit = 1
    while bit < size:
        if bit > 1:
            packed = jnp.concatenate([block_s, block_r], axis=0)
        got = lax.ppermute(packed, "ctx", [(q, q ^ bit) for q in range(size)])
        got_s, got_r = got[:states], got[states:]
        lower = (me // bit) % 2 == 0
        after_s = jnp.where(lower, after_s + jnp.exp(decay_rate * after_r) * got_s, after_s)
        after_r = jnp.where(lower, after_r + got_r, after_r)
        first_s = jnp.where(lower, block_s, got_s)
        first_r = jnp.where(lower, block_r, got_r)
        second_s = jnp.where(lower, got_s, block_s)
        block_s = first_s + jnp.exp(decay_rate * first_r) * second_s
        block_r = block_r + got_r
        bit *= 2
    return after_s


def exchange_sum(block, axis):
    size = lax.axis_size(axis)
    rows, columns = block.shape
    pieces = jnp.transpose(block.reshape(rows, size, columns // size), (1, 0, 2))
    got = lax.all_to_all(pieces, axis, 0, 0, tiled=True)
    return jnp.sum(got, axis=0)


def shards(scan_grad, step_size, scan_input, state_in, state_out, decay_rate, skip_gain):
    rows = scan_grad.shape[0]
    states = state_in.shape[1]
    in_b = jnp.transpose(state_in)
    out_b = jnp.transpose(state_out)
    packed = shard_summary(scan_grad, step_size, out_b, decay_rate)
    carried = carry_in(packed, decay_rate)
    scan_input_grad, b_t = shard_sweep(
        scan_grad, step_size, scan_input, in_b, out_b, decay_rate, skip_gain[None, :], carried,
        1.0 / math.sqrt(scan_grad.shape[1] * lax.axis_size("exp")),
    )
    b_term = b_t
    state_in_grad = exchange_sum(b_term, "exp")
    return (scan_input_grad, state_in_grad)


def solution(mesh):
    in_specs = (
        P("ctx", "exp"),
        P("ctx", "exp"),
        P("ctx", "exp"),
        P("ctx", None),
        P("ctx", None),
        P(None, "exp"),
        P("exp"),
    )
    out_specs = (P("ctx", "exp"), P(None, ("ctx", "exp")))
    return jax.shard_map(shards, mesh=mesh, in_specs=in_specs, out_specs=out_specs, check_vma=False)
```

```python
import math

import jax
import jax.numpy as jnp
from jax import lax
from jax.experimental import pallas as pl
from jax.experimental.pallas import tpu as pltpu
from jax.sharding import PartitionSpec as P

LANES = 128
LOG2_E = 1.4426950408889634


def tiled(column_block, tiles):
    return jnp.concatenate([column_block] * tiles, axis=1)


def lane_column(block, j, channels):
    lane = lax.broadcasted_iota(jnp.int32, block.shape, 1)
    column = jnp.sum(jnp.where(lane == j, block, 0.0), axis=1, keepdims=True)
    return jnp.broadcast_to(column, (block.shape[0], channels))


def summary_kernel(g_ref, s_ref, outt_ref, a_ref, out_ref, gf, sf):
    rows, channels = g_ref.shape
    states = a_ref.shape[0]
    gf[...] = g_ref[...].astype(jnp.float32)
    sf[...] = s_ref[...].astype(jnp.float32)
    out_ref[states:, :] = jnp.sum(sf[...], axis=0, keepdims=True)
    a = a_ref[...] * LOG2_E

    def run_block(base, incoming):
        out_block = outt_ref[:, base:base + LANES]

        def body(i, incoming):
            j = LANES - 1 - i
            t = base + j
            g_row = gf[pl.ds(t, 1), :]
            s_row = sf[pl.ds(t, 1), :]
            adjoint = lane_column(out_block, j, channels) * g_row + incoming
            return jnp.exp2(s_row * a) * adjoint

        return lax.fori_loop(0, LANES, body, incoming, unroll=32)

    incoming = jnp.zeros(a.shape, jnp.float32)
    for block in range(rows // LANES - 1, -1, -1):
        incoming = run_block(block * LANES, incoming)
    out_ref[0:states, :] = incoming


def sweep_kernel(
    g_ref, s_ref, x_ref, int_ref, outt_ref, a_ref, skip_ref, inc_ref,
    res_ref, bt_ref, gf, sf, wf, rf,
):
    rows, channels = g_ref.shape
    states = a_ref.shape[0]
    tiles = channels // LANES
    gf[...] = g_ref[...].astype(jnp.float32)
    sf[...] = s_ref[...].astype(jnp.float32)
    wf[...] = sf[...] * x_ref[...].astype(jnp.float32)
    a = a_ref[...] * LOG2_E
    skip = skip_ref[...]
    lane = lax.broadcasted_iota(jnp.int32, (states, LANES), 1)

    def run_block(base, incoming):
        in_block = int_ref[:, base:base + LANES]
        out_block = outt_ref[:, base:base + LANES]

        def body(i, carry):
            incoming, gathered = carry
            j = LANES - 1 - i
            t = base + j
            g_row = gf[pl.ds(t, 1), :]
            s_row = sf[pl.ds(t, 1), :]
            w_row = wf[pl.ds(t, 1), :]
            adjoint = lane_column(out_block, j, channels) * g_row + incoming
            mixed = jnp.sum(lane_column(in_block, j, channels) * adjoint, axis=0, keepdims=True)
            rf[pl.ds(t, 1), :] = s_row * mixed + skip * g_row
            weighted = adjoint * w_row
            part = weighted[:, 0:LANES]
            for k in range(1, tiles):
                part = part + weighted[:, k * LANES:(k + 1) * LANES]
            column = jnp.sum(part, axis=1, keepdims=True)
            gathered = jnp.where(lane == j, column, gathered)
            return (jnp.exp2(s_row * a) * adjoint, gathered)

        start = (incoming, jnp.zeros((states, LANES), jnp.float32))
        incoming, gathered = lax.fori_loop(0, LANES, body, start, unroll=32)
        bt_ref[:, base:base + LANES] = gathered
        return incoming

    incoming = inc_ref[...]
    for block in range(rows // LANES - 1, -1, -1):
        incoming = run_block(block * LANES, incoming)
    res_ref[...] = rf[...].astype(res_ref.dtype)


def vmem_spec():
    return pl.BlockSpec(memory_space=pltpu.VMEM)


def shard_summary(scan_grad, step_size, out_b, decay_rate):
    rows, channels = scan_grad.shape
    states = decay_rate.shape[0]
    return pl.pallas_call(
        summary_kernel,
        out_shape=jax.ShapeDtypeStruct((states + 1, channels), jnp.float32),
        in_specs=[vmem_spec()] * 4,
        out_specs=vmem_spec(),
        scratch_shapes=[pltpu.VMEM((rows, channels), jnp.float32)] * 2,
        cost_estimate=pl.CostEstimate(
            flops=6 * rows * decay_rate.size,
            transcendentals=rows * decay_rate.size,
            bytes_accessed=4 * rows * channels + 4 * out_b.size,
        ),
    )(scan_grad, step_size, out_b, decay_rate)


def shard_sweep(scan_grad, step_size, scan_input, in_b, out_b, decay_rate, skip_gain, incoming):
    rows, channels = scan_grad.shape
    states = decay_rate.shape[0]
    return pl.pallas_call(
        sweep_kernel,
        out_shape=(
            jax.ShapeDtypeStruct((rows, channels), jnp.bfloat16),
            jax.ShapeDtypeStruct((states, rows), jnp.float32),
        ),
        in_specs=[vmem_spec()] * 8,
        out_specs=(vmem_spec(), vmem_spec()),
        scratch_shapes=[pltpu.VMEM((rows, channels), jnp.float32)] * 4,
        cost_estimate=pl.CostEstimate(
            flops=12 * rows * decay_rate.size,
            transcendentals=rows * decay_rate.size,
            bytes_accessed=8 * rows * channels + 4 * (in_b.size + out_b.size) * 2,
        ),
    )(scan_grad, step_size, scan_input, in_b, out_b, decay_rate, skip_gain, incoming)


def doubling_carry(summary, total, decay_rate):
    size = lax.axis_size("ctx")
    states = summary.shape[0]
    packed = jnp.concatenate([summary, total], axis=0)
    packed = lax.ppermute(packed, "ctx", [(q, q - 1) for q in range(1, size)])
    reach = 1
    while reach < size:
        got = lax.ppermute(packed, "ctx", [(q, q - reach) for q in range(reach, size)])
        own_s, own_r = packed[:states], packed[states:]
        new_s = own_s + jnp.exp(decay_rate * own_r) * got[:states]
        packed = jnp.concatenate([new_s, own_r + got[states:]], axis=0)
        reach *= 2
    return packed[:states]


def carry_in(packed, decay_rate):
    size = lax.axis_size("ctx")
    states = packed.shape[0] - 1
    if size & (size - 1):
        return doubling_carry(packed[:states], packed[states:], decay_rate)
    me = lax.axis_index("ctx")
    block_s, block_r = packed[:states], packed[states:]
    after_s, after_r = jnp.zeros_like(block_s), jnp.zeros_like(block_r)
    bit = 1
    while bit < size:
        if bit > 1:
            packed = jnp.concatenate([block_s, block_r], axis=0)
        got = lax.ppermute(packed, "ctx", [(q, q ^ bit) for q in range(size)])
        got_s, got_r = got[:states], got[states:]
        lower = (me // bit) % 2 == 0
        if bit == 1:
            after_s = jnp.where(lower, got_s, after_s)
            after_r = jnp.where(lower, got_r, after_r)
        else:
            after_s = jnp.where(lower, after_s + jnp.exp(decay_rate * after_r) * got_s, after_s)
            after_r = jnp.where(lower, after_r + got_r, after_r)
        first_s = jnp.where(lower, block_s, got_s)
        first_r = jnp.where(lower, block_r, got_r)
        second_s = jnp.where(lower, got_s, block_s)
        block_s = first_s + jnp.exp(decay_rate * first_r) * second_s
        block_r = block_r + got_r
        bit *= 2
    return after_s


def exchange_sum(block, axis):
    size = lax.axis_size(axis)
    rows, columns = block.shape
    pieces = jnp.transpose(block.reshape(rows, size, columns // size), (1, 0, 2))
    got = lax.all_to_all(pieces, axis, 0, 0, tiled=True)
    return jnp.sum(got, axis=0)


def shards(scan_grad, step_size, scan_input, state_in, state_out, decay_rate, skip_gain):
    rows = scan_grad.shape[0]
    states = state_in.shape[1]
    in_b = jnp.transpose(state_in)
    out_b = jnp.transpose(state_out)
    packed = shard_summary(scan_grad, step_size, out_b, decay_rate)
    carried = carry_in(packed, decay_rate)
    scan_input_grad, b_t = shard_sweep(
        scan_grad, step_size, scan_input, in_b, out_b, decay_rate, skip_gain[None, :], carried
    )
    all_channels = scan_grad.shape[1] * lax.axis_size("exp")
    b_term = b_t * (1.0 / math.sqrt(all_channels))
    state_in_grad = exchange_sum(b_term, "exp")
    return (scan_input_grad, state_in_grad)


def solution(mesh):
    in_specs = (
        P("ctx", "exp"),
        P("ctx", "exp"),
        P("ctx", "exp"),
        P("ctx", None),
        P("ctx", None),
        P(None, "exp"),
        P("exp"),
    )
    out_specs = (P("ctx", "exp"), P(None, ("ctx", "exp")))
    return jax.shard_map(shards, mesh=mesh, in_specs=in_specs, out_specs=out_specs, check_vma=False)
```

```python
import math

import jax
import jax.numpy as jnp
from jax import lax
from jax.experimental import pallas as pl
from jax.experimental.pallas import tpu as pltpu
from jax.sharding import PartitionSpec as P

LANES = 128
LOG2_E = 1.4426950408889634


def tiled(column_block, tiles):
    return jnp.concatenate([column_block] * tiles, axis=1)


def lane_column(block, j, channels):
    lane = lax.broadcasted_iota(jnp.int32, block.shape, 1)
    column = jnp.sum(jnp.where(lane == j, block, 0.0), axis=1, keepdims=True)
    return jnp.broadcast_to(column, (block.shape[0], channels))


def summary_kernel(g_ref, s_ref, outt_ref, a_ref, out_ref, gf, sf):
    rows, channels = g_ref.shape
    states = a_ref.shape[0]
    gf[...] = g_ref[...].astype(jnp.float32)
    sf[...] = s_ref[...].astype(jnp.float32)
    out_ref[states:, :] = jnp.sum(sf[...], axis=0, keepdims=True)
    a = a_ref[...] * LOG2_E

    def run_block(base, incoming):
        out_block = outt_ref[:, base:base + LANES]

        def body(i, incoming):
            j = LANES - 1 - i
            t = base + j
            g_row = gf[pl.ds(t, 1), :]
            s_row = sf[pl.ds(t, 1), :]
            adjoint = lane_column(out_block, j, channels) * g_row + incoming
            return jnp.exp2(s_row * a) * adjoint

        return lax.fori_loop(0, LANES, body, incoming, unroll=LANES)

    incoming = jnp.zeros(a.shape, jnp.float32)
    for block in range(rows // LANES - 1, -1, -1):
        incoming = run_block(block * LANES, incoming)
    out_ref[0:states, :] = incoming


def sweep_kernel(
    g_ref, s_ref, x_ref, int_ref, outt_ref, a_ref, skip_ref, inc_ref,
    res_ref, bt_ref, gf, sf, wf, rf,
):
    rows, channels = g_ref.shape
    states = a_ref.shape[0]
    tiles = channels // LANES
    gf[...] = g_ref[...].astype(jnp.float32)
    sf[...] = s_ref[...].astype(jnp.float32)
    wf[...] = sf[...] * x_ref[...].astype(jnp.float32)
    a = a_ref[...] * LOG2_E
    skip = skip_ref[...]
    lane = lax.broadcasted_iota(jnp.int32, (states, LANES), 1)

    def run_block(base, incoming):
        in_block = int_ref[:, base:base + LANES]
        out_block = outt_ref[:, base:base + LANES]

        def body(i, carry):
            incoming, gathered = carry
            j = LANES - 1 - i
            t = base + j
            g_row = gf[pl.ds(t, 1), :]
            s_row = sf[pl.ds(t, 1), :]
            w_row = wf[pl.ds(t, 1), :]
            adjoint = lane_column(out_block, j, channels) * g_row + incoming
            mixed = jnp.sum(lane_column(in_block, j, channels) * adjoint, axis=0, keepdims=True)
            rf[pl.ds(t, 1), :] = s_row * mixed + skip * g_row
            weighted = adjoint * w_row
            part = weighted[:, 0:LANES]
            for k in range(1, tiles):
                part = part + weighted[:, k * LANES:(k + 1) * LANES]
            column = jnp.sum(part, axis=1, keepdims=True)
            gathered = jnp.where(lane == j, column, gathered)
            return (jnp.exp2(s_row * a) * adjoint, gathered)

        start = (incoming, jnp.zeros((states, LANES), jnp.float32))
        incoming, gathered = lax.fori_loop(0, LANES, body, start, unroll=32)
        bt_ref[:, base:base + LANES] = gathered
        return incoming

    incoming = inc_ref[...]
    for block in range(rows // LANES - 1, -1, -1):
        incoming = run_block(block * LANES, incoming)
    res_ref[...] = rf[...].astype(res_ref.dtype)


def vmem_spec():
    return pl.BlockSpec(memory_space=pltpu.VMEM)


def shard_summary(scan_grad, step_size, out_b, decay_rate):
    rows, channels = scan_grad.shape
    states = decay_rate.shape[0]
    return pl.pallas_call(
        summary_kernel,
        out_shape=jax.ShapeDtypeStruct((states + 1, channels), jnp.float32),
        in_specs=[vmem_spec()] * 4,
        out_specs=vmem_spec(),
        scratch_shapes=[pltpu.VMEM((rows, channels), jnp.float32)] * 2,
        cost_estimate=pl.CostEstimate(
            flops=6 * rows * decay_rate.size,
            transcendentals=rows * decay_rate.size,
            bytes_accessed=4 * rows * channels + 4 * out_b.size,
        ),
    )(scan_grad, step_size, out_b, decay_rate)


def shard_sweep(scan_grad, step_size, scan_input, in_b, out_b, decay_rate, skip_gain, incoming):
    rows, channels = scan_grad.shape
    states = decay_rate.shape[0]
    return pl.pallas_call(
        sweep_kernel,
        out_shape=(
            jax.ShapeDtypeStruct((rows, channels), jnp.bfloat16),
            jax.ShapeDtypeStruct((states, rows), jnp.float32),
        ),
        in_specs=[vmem_spec()] * 8,
        out_specs=(vmem_spec(), vmem_spec()),
        scratch_shapes=[pltpu.VMEM((rows, channels), jnp.float32)] * 4,
        cost_estimate=pl.CostEstimate(
            flops=12 * rows * decay_rate.size,
            transcendentals=rows * decay_rate.size,
            bytes_accessed=8 * rows * channels + 4 * (in_b.size + out_b.size) * 2,
        ),
    )(scan_grad, step_size, scan_input, in_b, out_b, decay_rate, skip_gain, incoming)


def doubling_carry(summary, total, decay_rate):
    size = lax.axis_size("ctx")
    states = summary.shape[0]
    packed = jnp.concatenate([summary, total], axis=0)
    packed = lax.ppermute(packed, "ctx", [(q, q - 1) for q in range(1, size)])
    reach = 1
    while reach < size:
        got = lax.ppermute(packed, "ctx", [(q, q - reach) for q in range(reach, size)])
        own_s, own_r = packed[:states], packed[states:]
        new_s = own_s + jnp.exp(decay_rate * own_r) * got[:states]
        packed = jnp.concatenate([new_s, own_r + got[states:]], axis=0)
        reach *= 2
    return packed[:states]


def carry_in(packed, decay_rate):
    size = lax.axis_size("ctx")
    states = packed.shape[0] - 1
    if size & (size - 1):
        return doubling_carry(packed[:states], packed[states:], decay_rate)
    me = lax.axis_index("ctx")
    block_s, block_r = packed[:states], packed[states:]
    after_s, after_r = jnp.zeros_like(block_s), jnp.zeros_like(block_r)
    bit = 1
    while bit < size:
        if bit > 1:
            packed = jnp.concatenate([block_s, block_r], axis=0)
        got = lax.ppermute(packed, "ctx", [(q, q ^ bit) for q in range(size)])
        got_s, got_r = got[:states], got[states:]
        lower = (me // bit) % 2 == 0
        if bit == 1:
            after_s = jnp.where(lower, got_s, after_s)
            after_r = jnp.where(lower, got_r, after_r)
        else:
            after_s = jnp.where(lower, after_s + jnp.exp(decay_rate * after_r) * got_s, after_s)
            after_r = jnp.where(lower, after_r + got_r, after_r)
        first_s = jnp.where(lower, block_s, got_s)
        first_r = jnp.where(lower, block_r, got_r)
        second_s = jnp.where(lower, got_s, block_s)
        block_s = first_s + jnp.exp(decay_rate * first_r) * second_s
        block_r = block_r + got_r
        bit *= 2
    return after_s


def exchange_sum(block, axis):
    size = lax.axis_size(axis)
    rows, columns = block.shape
    pieces = jnp.transpose(block.reshape(rows, size, columns // size), (1, 0, 2))
    got = lax.all_to_all(pieces, axis, 0, 0, tiled=True)
    return jnp.sum(got, axis=0)


def shards(scan_grad, step_size, scan_input, state_in, state_out, decay_rate, skip_gain):
    rows = scan_grad.shape[0]
    states = state_in.shape[1]
    in_b = jnp.transpose(state_in)
    out_b = jnp.transpose(state_out)
    packed = shard_summary(scan_grad, step_size, out_b, decay_rate)
    carried = carry_in(packed, decay_rate)
    scan_input_grad, b_t = shard_sweep(
        scan_grad, step_size, scan_input, in_b, out_b, decay_rate, skip_gain[None, :], carried
    )
    all_channels = scan_grad.shape[1] * lax.axis_size("exp")
    b_term = b_t * (1.0 / math.sqrt(all_channels))
    state_in_grad = exchange_sum(b_term, "exp")
    return (scan_input_grad, state_in_grad)


def solution(mesh):
    in_specs = (
        P("ctx", "exp"),
        P("ctx", "exp"),
        P("ctx", "exp"),
        P("ctx", None),
        P("ctx", None),
        P(None, "exp"),
        P("exp"),
    )
    out_specs = (P("ctx", "exp"), P(None, ("ctx", "exp")))
    return jax.shard_map(shards, mesh=mesh, in_specs=in_specs, out_specs=out_specs, check_vma=False)
```

```python
import math

import jax
import jax.numpy as jnp
from jax import lax
from jax.experimental import pallas as pl
from jax.experimental.pallas import tpu as pltpu
from jax.sharding import PartitionSpec as P

LANES = 128
LOG2_E = 1.4426950408889634


def tiled(column_block, tiles):
    return jnp.concatenate([column_block] * tiles, axis=1)


def lane_column(block, j, channels):
    lane = lax.broadcasted_iota(jnp.int32, block.shape, 1)
    column = jnp.sum(jnp.where(lane == j, block, 0.0), axis=1, keepdims=True)
    return jnp.broadcast_to(column, (block.shape[0], channels))


def summary_kernel(g_ref, s_ref, outt_ref, a_ref, out_ref, gf, sf):
    rows, channels = g_ref.shape
    states = a_ref.shape[0]
    gf[...] = g_ref[...].astype(jnp.float32)
    sf[...] = s_ref[...].astype(jnp.float32)
    out_ref[states:, :] = jnp.sum(sf[...], axis=0, keepdims=True)
    a = a_ref[...] * LOG2_E

    def run_block(base, incoming):
        out_block = outt_ref[:, base:base + LANES]

        def body(i, incoming):
            j = LANES - 1 - i
            t = base + j
            g_row = gf[pl.ds(t, 1), :]
            s_row = sf[pl.ds(t, 1), :]
            adjoint = lane_column(out_block, j, channels) * g_row + incoming
            return jnp.exp2(s_row * a) * adjoint

        return lax.fori_loop(0, LANES, body, incoming, unroll=32)

    incoming = jnp.zeros(a.shape, jnp.float32)
    for block in range(rows // LANES - 1, -1, -1):
        incoming = run_block(block * LANES, incoming)
    out_ref[0:states, :] = incoming


def sweep_kernel(
    g_ref, s_ref, x_ref, int_ref, outt_ref, a_ref, skip_ref, inc_ref,
    res_ref, bt_ref, gf, sf, wf, rf,
):
    rows, channels = g_ref.shape
    states = a_ref.shape[0]
    tiles = channels // LANES
    gf[...] = g_ref[...].astype(jnp.float32)
    sf[...] = s_ref[...].astype(jnp.float32)
    wf[...] = sf[...] * x_ref[...].astype(jnp.float32)
    a = a_ref[...] * LOG2_E
    skip = skip_ref[...]
    lane = lax.broadcasted_iota(jnp.int32, (states, LANES), 1)

    def run_block(base, incoming):
        in_block = int_ref[:, base:base + LANES]
        out_block = outt_ref[:, base:base + LANES]

        def body(i, carry):
            incoming, gathered = carry
            j = LANES - 1 - i
            t = base + j
            g_row = gf[pl.ds(t, 1), :]
            s_row = sf[pl.ds(t, 1), :]
            w_row = wf[pl.ds(t, 1), :]
            adjoint = lane_column(out_block, j, channels) * g_row + incoming
            mixed = jnp.sum(lane_column(in_block, j, channels) * adjoint, axis=0, keepdims=True)
            rf[pl.ds(t, 1), :] = s_row * mixed + skip * g_row
            weighted = adjoint * w_row
            part = weighted[:, 0:LANES]
            for k in range(1, tiles):
                part = part + weighted[:, k * LANES:(k + 1) * LANES]
            column = jnp.sum(part, axis=1, keepdims=True)
            gathered = jnp.where(lane == j, column, gathered)
            return (jnp.exp2(s_row * a) * adjoint, gathered)

        start = (incoming, jnp.zeros((states, LANES), jnp.float32))
        incoming, gathered = lax.fori_loop(0, LANES, body, start, unroll=64)
        bt_ref[:, base:base + LANES] = gathered
        return incoming

    incoming = inc_ref[...]
    for block in range(rows // LANES - 1, -1, -1):
        incoming = run_block(block * LANES, incoming)
    res_ref[...] = rf[...].astype(res_ref.dtype)


def vmem_spec():
    return pl.BlockSpec(memory_space=pltpu.VMEM)


def shard_summary(scan_grad, step_size, out_b, decay_rate):
    rows, channels = scan_grad.shape
    states = decay_rate.shape[0]
    return pl.pallas_call(
        summary_kernel,
        out_shape=jax.ShapeDtypeStruct((states + 1, channels), jnp.float32),
        in_specs=[vmem_spec()] * 4,
        out_specs=vmem_spec(),
        scratch_shapes=[pltpu.VMEM((rows, channels), jnp.float32)] * 2,
        cost_estimate=pl.CostEstimate(
            flops=6 * rows * decay_rate.size,
            transcendentals=rows * decay_rate.size,
            bytes_accessed=4 * rows * channels + 4 * out_b.size,
        ),
    )(scan_grad, step_size, out_b, decay_rate)


def shard_sweep(scan_grad, step_size, scan_input, in_b, out_b, decay_rate, skip_gain, incoming):
    rows, channels = scan_grad.shape
    states = decay_rate.shape[0]
    return pl.pallas_call(
        sweep_kernel,
        out_shape=(
            jax.ShapeDtypeStruct((rows, channels), jnp.bfloat16),
            jax.ShapeDtypeStruct((states, rows), jnp.float32),
        ),
        in_specs=[vmem_spec()] * 8,
        out_specs=(vmem_spec(), vmem_spec()),
        scratch_shapes=[pltpu.VMEM((rows, channels), jnp.float32)] * 4,
        cost_estimate=pl.CostEstimate(
            flops=12 * rows * decay_rate.size,
            transcendentals=rows * decay_rate.size,
            bytes_accessed=8 * rows * channels + 4 * (in_b.size + out_b.size) * 2,
        ),
    )(scan_grad, step_size, scan_input, in_b, out_b, decay_rate, skip_gain, incoming)


def doubling_carry(summary, total, decay_rate):
    size = lax.axis_size("ctx")
    states = summary.shape[0]
    packed = jnp.concatenate([summary, total], axis=0)
    packed = lax.ppermute(packed, "ctx", [(q, q - 1) for q in range(1, size)])
    reach = 1
    while reach < size:
        got = lax.ppermute(packed, "ctx", [(q, q - reach) for q in range(reach, size)])
        own_s, own_r = packed[:states], packed[states:]
        new_s = own_s + jnp.exp(decay_rate * own_r) * got[:states]
        packed = jnp.concatenate([new_s, own_r + got[states:]], axis=0)
        reach *= 2
    return packed[:states]


def carry_in(packed, decay_rate):
    size = lax.axis_size("ctx")
    states = packed.shape[0] - 1
    if size & (size - 1):
        return doubling_carry(packed[:states], packed[states:], decay_rate)
    me = lax.axis_index("ctx")
    block_s, block_r = packed[:states], packed[states:]
    after_s, after_r = jnp.zeros_like(block_s), jnp.zeros_like(block_r)
    bit = 1
    while bit < size:
        if bit > 1:
            packed = jnp.concatenate([block_s, block_r], axis=0)
        got = lax.ppermute(packed, "ctx", [(q, q ^ bit) for q in range(size)])
        got_s, got_r = got[:states], got[states:]
        lower = (me // bit) % 2 == 0
        if bit == 1:
            after_s = jnp.where(lower, got_s, after_s)
            after_r = jnp.where(lower, got_r, after_r)
        else:
            after_s = jnp.where(lower, after_s + jnp.exp(decay_rate * after_r) * got_s, after_s)
            after_r = jnp.where(lower, after_r + got_r, after_r)
        first_s = jnp.where(lower, block_s, got_s)
        first_r = jnp.where(lower, block_r, got_r)
        second_s = jnp.where(lower, got_s, block_s)
        block_s = first_s + jnp.exp(decay_rate * first_r) * second_s
        block_r = block_r + got_r
        bit *= 2
    return after_s


def exchange_sum(block, axis):
    size = lax.axis_size(axis)
    rows, columns = block.shape
    pieces = jnp.transpose(block.reshape(rows, size, columns // size), (1, 0, 2))
    got = lax.all_to_all(pieces, axis, 0, 0, tiled=True)
    return jnp.sum(got, axis=0)


def shards(scan_grad, step_size, scan_input, state_in, state_out, decay_rate, skip_gain):
    rows = scan_grad.shape[0]
    states = state_in.shape[1]
    in_b = jnp.transpose(state_in)
    out_b = jnp.transpose(state_out)
    packed = shard_summary(scan_grad, step_size, out_b, decay_rate)
    carried = carry_in(packed, decay_rate)
    scan_input_grad, b_t = shard_sweep(
        scan_grad, step_size, scan_input, in_b, out_b, decay_rate, skip_gain[None, :], carried
    )
    all_channels = scan_grad.shape[1] * lax.axis_size("exp")
    b_term = b_t * (1.0 / math.sqrt(all_channels))
    state_in_grad = exchange_sum(b_term, "exp")
    return (scan_input_grad, state_in_grad)


def solution(mesh):
    in_specs = (
        P("ctx", "exp"),
        P("ctx", "exp"),
        P("ctx", "exp"),
        P("ctx", None),
        P("ctx", None),
        P(None, "exp"),
        P("exp"),
    )
    out_specs = (P("ctx", "exp"), P(None, ("ctx", "exp")))
    return jax.shard_map(shards, mesh=mesh, in_specs=in_specs, out_specs=out_specs, check_vma=False)
```
